32 devices in a mesh: grp: 2 (over y), cand: 4 (over z), head: 2 (over x), hist: 2 (over core).
Axes of the slice: x: 2, y: 2, z: 4, core: 2. Of those that a mesh axis runs over, the one named last changes fastest.
Arguments:
- candidates: bfloat16 [4, 1024, 1024], P('grp', 'cand'), parts along dimension 0, may hold values from -6 to 6
- w_in: bfloat16 [1024, 2, 1024], P(None, None, 'head'), may hold values from -0.1875 to 0.1875
- w_out: bfloat16 [1024, 1024], P('head'), may hold values from -0.1875 to 0.1875
- hist_keys: bfloat16 [4, 16384, 1024], P('grp', ('cand', 'hist'), 'head'), parts along dimension 0, may hold values from -6 to 6
- hist_values: bfloat16 [4, 16384, 1024], P('grp', ('cand', 'hist'), 'head'), parts along dimension 0, may hold values from -48 to 48
- lengths: int32 [4], P('grp'), parts along dimension 0, may hold values from 2048 to 16384, as said below
- counts: int32 [4], P('grp'), parts along dimension 0, may hold values from 256 to 1024, as said below
Outputs:
- ranked: bfloat16 [4, 1024, 1024], P('grp', 'cand', 'head'), parts along dimension 0
The draws below stay inside these ranges and needn't reach their ends.
There are 2 independent parts, one for each index of `grp`. The reference program is written for one: setup_inputs(seed, part) draws one part's arguments, and reference() takes and returns one part's arrays. A program takes and returns all parts, laid end to end along the dimension named above; an argument that names none is the same for every part. Nothing has to cross between parts.
Inputs may be any that keep to these rules, and one draw needn't show every extreme that they name: `lengths`: in every draw some request has exactly 16384 history positions. `counts`: in every draw some request has all 1024 candidates live.
All inputs are finite; a program needn't handle non-finite values.
Results may differ from the reference program's by a relative error of at most 0.0057.
Values may be sent and summed in bfloat16 or wider, within the bound.
No kernel may reach another device: no remote copies, remote signals or barrier semaphores. Data moves between devices by JAX's collectives and lax.ppermute only.
A program may use at most 64 MiB of HBM per device.

```python
import math
import jax
import jax.numpy as jnp
from jax import lax

D = 1024
HEADS = 16
HMAX = 16384
REQ = 2
CANDS = 1024


def draw_hist_values(key, part):
    shape = (REQ, HMAX, D)
    base = jax.random.normal(jax.random.fold_in(key, 11), shape, jnp.float32)
    spread = jnp.exp(jax.random.uniform(jax.random.fold_in(key, 12), (D,), jnp.float32, math.log(0.5), math.log(5.0)))
    rising = 3.0 ** (jnp.arange(D, dtype=jnp.float32) / D)
    return jnp.clip(base * spread * rising, -48.0, 48.0).astype(jnp.bfloat16)


def draw_lengths(key, part):
    drawn = jax.random.randint(jax.random.fold_in(key, 21), (REQ,), HMAX // 8, HMAX, dtype=jnp.int32)
    longest = jnp.asarray(part, jnp.int32) % REQ
    return jnp.where(jnp.arange(REQ, dtype=jnp.int32) == longest, HMAX, drawn).astype(jnp.int32)


def draw_counts(key, part):
    drawn = jax.random.randint(jax.random.fold_in(key, 31), (REQ,), CANDS // 4, CANDS, dtype=jnp.int32)
    fullest = jnp.asarray(part, jnp.int32) % REQ
    return jnp.where(jnp.arange(REQ, dtype=jnp.int32) == fullest, CANDS, drawn).astype(jnp.int32)


def block_levels(rng, extent, shards, least, largest):
    def one(position, shards_of):
        draws = jax.random.uniform(jax.random.fold_in(jax.random.fold_in(rng, 6), position), (shards_of,), jnp.float32, least / len(shards), largest / len(shards))
        return jnp.repeat(jnp.exp(draws), extent[position] // shards_of).reshape((-1,) + (1,) * (len(extent) - position - 1))

    level = one(*shards[0])
    for cut in shards[1:]:
        level = level * one(*cut)
    return level


def normal_values(rng, dims, deviation, reach, shards=(), kind=jnp.bfloat16):
    factor_of = block_levels(rng, dims, shards, -0.22, 0.18) if shards else 1.0
    values = jax.random.normal(rng, dims, jnp.float32) * deviation * factor_of
    return jnp.minimum(jnp.maximum(values, -reach), reach).astype(kind)


def setup_inputs(seed: int = 0, part: int = 0) -> dict:
    arg_keys = jax.random.split(jax.random.key(seed), 8)
    part_keys = jax.random.split(jax.random.fold_in(arg_keys[7], part), 8)
    return {
        "candidates": normal_values(part_keys[0], (REQ, CANDS, D), 1.0, 6.0, ((1, 4),)),
        "w_in": normal_values(arg_keys[1], (D, 2, D), D ** -0.5, 0.1875, ((2, 2),)),
        "w_out": normal_values(arg_keys[2], (D, D), D ** -0.5, 0.1875, ((0, 2),)),
        "hist_keys": normal_values(part_keys[3], (REQ, HMAX, D), 1.0, 6.0, ((1, 8), (2, 2))),
        "hist_values": draw_hist_values(jax.random.fold_in(jax.random.fold_in(arg_keys[7], part), 71), part),
        "lengths": draw_lengths(jax.random.fold_in(jax.random.fold_in(arg_keys[7], part), 71), part),
        "counts": draw_counts(jax.random.fold_in(jax.random.fold_in(arg_keys[7], part), 71), part),
    }


def layer_norm_rows(values, width):
    row_mean = lax.optimization_barrier(jnp.sum(values, axis=-1, keepdims=True)) / width
    row_square = lax.optimization_barrier(jnp.sum(values * values, axis=-1, keepdims=True)) / width
    return (values - row_mean) * lax.rsqrt(row_square - row_mean * row_mean + 1e-05)

def reference(candidates, w_in, w_out, hist_keys, hist_values, lengths, counts):
    head_dim = D // HEADS
    score_scale = 1.0 / math.sqrt(head_dim)
    cand_wide = candidates.astype(jnp.float32)
    normed = layer_norm_rows(cand_wide, D).astype(jnp.bfloat16)
    projected = jnp.dot(normed.reshape(REQ * CANDS, D), w_in.reshape(D, 2 * D), preferred_element_type=jnp.float32)
    activated = jax.nn.silu(projected).astype(jnp.bfloat16).reshape(REQ, CANDS, 2, D)
    gate_u = activated[:, :, 0, :]
    query_heads = activated[:, :, 1, :].astype(jnp.float32).reshape(REQ, CANDS, HEADS, head_dim)
    block_len = math.gcd(HMAX, 512)
    block_count = HMAX // block_len
    key_blocks = hist_keys.reshape(REQ, block_count, block_len, HEADS, head_dim).transpose(1, 0, 2, 3, 4)
    value_blocks = hist_values.reshape(REQ, block_count, block_len, HEADS, head_dim).transpose(1, 0, 2, 3, 4)
    offsets = jnp.arange(block_len, dtype=jnp.int32)

    def advance(running, inputs):
        key_block, value_block, block_index = inputs
        positions = block_index * block_len + offsets
        scores = jnp.einsum('rche,rjhe->rchj', query_heads, key_block.astype(jnp.float32)) * score_scale
        in_range = positions[None, :] < lengths[:, None]
        weights = jnp.where(in_range[:, None, None, :], jax.nn.silu(scores), 0.0).astype(jnp.bfloat16)
        update = jnp.einsum('rchj,rjhe->rche', weights.astype(jnp.float32), value_block.astype(jnp.float32))
        return (running + update, None)
    running = jnp.zeros((REQ, CANDS, HEADS, head_dim), jnp.float32)
    running, _ = lax.scan(advance, running, (key_blocks, value_blocks, jnp.arange(block_count, dtype=jnp.int32)))
    attended = running.reshape(REQ, CANDS, D) / lengths.astype(jnp.float32)[:, None, None]
    gated = (layer_norm_rows(attended, D) * gate_u.astype(jnp.float32)).astype(jnp.bfloat16)
    projected_out = jnp.dot(gated.reshape(REQ * CANDS, D), w_out, preferred_element_type=jnp.float32)
    summed = cand_wide + projected_out.reshape(REQ, CANDS, D)
    row_ids = jnp.arange(CANDS, dtype=jnp.int32)
    in_count = row_ids[None, :] < counts[:, None]
    return jnp.where(in_count[:, :, None], summed, 0.0).astype(jnp.bfloat16)
```

```python
import math

import jax
import jax.numpy as jnp
from jax import lax
from jax.sharding import PartitionSpec as P

HEADS = 16


def layer_norm_rows(values, width):
    row_mean = jnp.sum(values, axis=-1, keepdims=True) / width
    row_square = jnp.sum(values * values, axis=-1, keepdims=True) / width
    return (values - row_mean) * lax.rsqrt(row_square - row_mean * row_mean + 1e-05)


def ring(n):
    return [(i, (i + 1) % n) for i in range(n)]


def swap(n):
    return [(i, n - 1 - i) for i in range(n)]


def attend(query_rows, key_block, value_block, valid, head_dim):
    row_count, width_here = query_rows.shape
    key_count = key_block.shape[0]
    heads_here = width_here // head_dim
    score_scale = 1.0 / math.sqrt(head_dim)
    query_heads = query_rows.reshape(row_count, heads_here, head_dim)
    key_heads = key_block.reshape(key_count, heads_here, head_dim)
    value_heads = value_block.reshape(key_count, heads_here, head_dim)
    scores = (
        jnp.einsum("che,jhe->chj", query_heads, key_heads, preferred_element_type=jnp.float32)
        * score_scale
    )
    weights = jnp.where(valid[None, None, :], jax.nn.silu(scores), 0.0).astype(jnp.bfloat16)
    mixed_heads = jnp.einsum("chj,jhe->che", weights, value_heads, preferred_element_type=jnp.float32)
    return mixed_heads.reshape(row_count, width_here)


def ring_reduce_scatter(chunks, axis, n, index):
    acc = None
    for t in range(1, n):
        part = lax.dynamic_index_in_dim(chunks, (index - t) % n, 0, keepdims=False)
        if acc is not None:
            part = part + acc.astype(jnp.float32)
        acc = lax.ppermute(part.astype(jnp.bfloat16), axis, ring(n))
    own = lax.dynamic_index_in_dim(chunks, index, 0, keepdims=False)
    return own if acc is None else own + acc.astype(jnp.float32)


def shards(candidates, w_in, w_out, hist_keys, hist_values, lengths, counts):
    requests, row_count, width = candidates.shape
    width_here = w_in.shape[2]
    head_dim = width // HEADS
    n_cand = lax.axis_size("cand")
    n_hist = lax.axis_size("hist")
    n_head = lax.axis_size("head")
    cand_index = lax.axis_index("cand")
    hist_index = lax.axis_index("hist")
    head_index = lax.axis_index("head")
    assert n_hist == 2 and requests == 2
    mine = hist_index
    other = 1 - hist_index

    cand_mine = lax.dynamic_index_in_dim(candidates, mine, 0, keepdims=False)
    cand_wide = cand_mine.astype(jnp.float32)
    normed = layer_norm_rows(cand_wide, width).astype(jnp.bfloat16)
    projected = jnp.dot(
        normed, w_in.reshape(width, 2 * width_here), preferred_element_type=jnp.float32
    )
    activated = jax.nn.silu(projected).astype(jnp.bfloat16).reshape(row_count, 2, width_here)
    gate_u = activated[:, 0, :]
    query_mine = activated[:, 1, :]

    blocks = hist_keys.shape[1]
    positions = (cand_index * n_hist + hist_index) * blocks + jnp.arange(blocks, dtype=jnp.int32)
    keys_mine = lax.dynamic_index_in_dim(hist_keys, mine, 0, keepdims=False)
    keys_other = lax.dynamic_index_in_dim(hist_keys, other, 0, keepdims=False)
    values_mine = lax.dynamic_index_in_dim(hist_values, mine, 0, keepdims=False)
    values_other = lax.dynamic_index_in_dim(hist_values, other, 0, keepdims=False)
    length_mine = lax.dynamic_index_in_dim(lengths, mine, 0, keepdims=False)
    length_other = lax.dynamic_index_in_dim(lengths, other, 0, keepdims=False)
    valid_mine = positions < length_mine
    valid_other = positions < length_other

    query_k = query_mine
    own_sum = None
    acc = None
    for k in range(n_cand):
        if k > 0:
            query_k = lax.ppermute(query_k, "cand", ring(n_cand))
        query_partner = lax.ppermute(query_k, "hist", swap(n_hist))
        part_other = attend(query_partner, keys_other, values_other, valid_other, head_dim)
        part_mine = attend(query_k, keys_mine, values_mine, valid_mine, head_dim)
        chip_sum = part_mine + lax.ppermute(part_other, "hist", swap(n_hist))
        if k == 0:
            own_sum = chip_sum
        else:
            if acc is not None:
                chip_sum = chip_sum + acc.astype(jnp.float32)
            acc = lax.ppermute(chip_sum.astype(jnp.bfloat16), "cand", ring(n_cand))
    total = own_sum if acc is None else own_sum + acc.astype(jnp.float32)

    attended = total / length_mine.astype(jnp.float32)
    moments = lax.psum(
        (jnp.sum(attended, axis=-1), jnp.sum(attended * attended, axis=-1)), "head"
    )
    row_mean = moments[0][..., None] / width
    row_square = moments[1][..., None] / width
    normed_out = (attended - row_mean) * lax.rsqrt(row_square - row_mean * row_mean + 1e-05)
    gated = (normed_out * gate_u.astype(jnp.float32)).astype(jnp.bfloat16)
    partial_out = jnp.dot(gated, w_out, preferred_element_type=jnp.float32)
    slice_width = width // n_head
    chunks = partial_out.reshape(row_count, n_head, slice_width).transpose(1, 0, 2)
    summed = ring_reduce_scatter(chunks, "head", n_head, head_index)
    residual = lax.dynamic_slice_in_dim(cand_wide, head_index * slice_width, slice_width, 1)
    row_ids = cand_index * row_count + jnp.arange(row_count, dtype=jnp.int32)
    count_mine = lax.dynamic_index_in_dim(counts, mine, 0, keepdims=False)
    result = jnp.where((row_ids < count_mine)[:, None], residual + summed, 0.0).astype(jnp.bfloat16)
    result_other = lax.ppermute(result, "hist", swap(n_hist))
    first = jnp.where(hist_index == 0, result, result_other)
    second = jnp.where(hist_index == 0, result_other, result)
    return jnp.stack([first, second])


def solution(mesh):
    in_specs = (
        P("grp", "cand", None),
        P(None, None, "head"),
        P("head", None),
        P("grp", ("cand", "hist"), "head"),
        P("grp", ("cand", "hist"), "head"),
        P("grp"),
        P("grp"),
    )
    out_specs = P("grp", "cand", "head")
    return jax.shard_map(shards, mesh=mesh, in_specs=in_specs, out_specs=out_specs, check_vma=False)
```

```python
import math

import jax
import jax.numpy as jnp
from jax import lax
from jax.sharding import PartitionSpec as P

HEADS = 16


def layer_norm_rows(values, width):
    row_mean = jnp.sum(values, axis=-1, keepdims=True) / width
    row_square = jnp.sum(values * values, axis=-1, keepdims=True) / width
    return (values - row_mean) * lax.rsqrt(row_square - row_mean * row_mean + 1e-05)


def ring(n):
    return [(i, (i + 1) % n) for i in range(n)]


def swap(n):
    return [(i, n - 1 - i) for i in range(n)]


def attend(query_t, key_block, value_block, valid, head_dim):
    width_here, row_count = query_t.shape
    key_count = key_block.shape[0]
    heads_here = width_here // head_dim
    half_scale = 0.5 / math.sqrt(head_dim)
    query_heads = query_t.reshape(heads_here, head_dim, row_count)
    key_heads = key_block.reshape(key_count, heads_here, head_dim)
    value_heads = value_block.reshape(key_count, heads_here, head_dim)
    halves = (
        jnp.einsum("hec,jhe->hcj", query_heads, key_heads, preferred_element_type=jnp.float32)
        * half_scale
    )
    silu = halves + halves * jnp.tanh(halves)
    weights = jnp.where(valid[None, None, :], silu, 0.0).astype(jnp.bfloat16)
    return jnp.einsum("hcj,jhe->hce", weights, value_heads, preferred_element_type=jnp.float32)


def ring_reduce_scatter(chunks, axis, n, index):
    acc = None
    for t in range(1, n):
        part = lax.dynamic_index_in_dim(chunks, (index - t) % n, 0, keepdims=False)
        if acc is not None:
            part = part + acc.astype(jnp.float32)
        acc = lax.ppermute(part.astype(jnp.bfloat16), axis, ring(n))
    own = lax.dynamic_index_in_dim(chunks, index, 0, keepdims=False)
    return own if acc is None else own + acc.astype(jnp.float32)


def ring_sum(values, axis, n):
    total = values
    moving = values
    for _ in range(1, n):
        moving = lax.ppermute(moving, axis, ring(n))
        total = total + moving
    return total


def shards(candidates, w_in, w_out, hist_keys, hist_values, lengths, counts):
    requests, row_count, width = candidates.shape
    width_here = w_in.shape[2]
    head_dim = width // HEADS
    heads_here = width_here // head_dim
    n_cand = lax.axis_size("cand")
    n_hist = lax.axis_size("hist")
    n_head = lax.axis_size("head")
    cand_index = lax.axis_index("cand")
    hist_index = lax.axis_index("hist")
    head_index = lax.axis_index("head")
    assert n_hist == 2 and requests == 2
    first_core = hist_index == 0

    cand_mine = jnp.where(first_core, candidates[0], candidates[1])
    cand_wide = cand_mine.astype(jnp.float32)
    normed = layer_norm_rows(cand_wide, width).astype(jnp.bfloat16)
    projected = jnp.dot(
        normed, w_in.reshape(width, 2 * width_here), preferred_element_type=jnp.float32
    )
    activated = jax.nn.silu(projected).astype(jnp.bfloat16).reshape(row_count, 2, width_here)
    gate_u = activated[:, 0, :]
    query_t = activated[:, 1, :].T

    blocks = hist_keys.shape[1]
    positions = (cand_index * n_hist + hist_index) * blocks + jnp.arange(blocks, dtype=jnp.int32)
    valid = [positions < lengths[r] for r in range(requests)]

    query_k = query_t
    own_sum = None
    acc = None
    for k in range(n_cand):
        if k > 0:
            query_k = lax.ppermute(query_k, "cand", ring(n_cand))
        query_partner = lax.ppermute(query_k, "hist", swap(n_hist))
        query_r = (
            jnp.where(first_core, query_k, query_partner),
            jnp.where(first_core, query_partner, query_k),
        )
        parts = [
            attend(query_r[r], hist_keys[r], hist_values[r], valid[r], head_dim)
            for r in range(requests)
        ]
        keep = jnp.where(first_core, parts[0], parts[1])
        send = jnp.where(first_core, parts[1], parts[0])
        chip_sum = keep + lax.ppermute(send, "hist", swap(n_hist))
        if k == 0:
            own_sum = chip_sum
        else:
            if acc is not None:
                chip_sum = chip_sum + acc.astype(jnp.float32)
            acc = lax.ppermute(chip_sum.astype(jnp.bfloat16), "cand", ring(n_cand))
    total = own_sum if acc is None else own_sum + acc.astype(jnp.float32)

    length_mine = jnp.where(first_core, lengths[0], lengths[1])
    attended = total / length_mine.astype(jnp.float32)
    moments = ring_sum(
        jnp.stack([jnp.sum(attended, axis=(0, 2)), jnp.sum(attended * attended, axis=(0, 2))]),
        "head",
        n_head,
    )
    row_mean = moments[0][None, :, None] / width
    row_square = moments[1][None, :, None] / width
    normed_out = (attended - row_mean) * lax.rsqrt(row_square - row_mean * row_mean + 1e-05)
    gate_heads = gate_u.reshape(row_count, heads_here, head_dim).transpose(1, 0, 2)
    gated = (normed_out * gate_heads.astype(jnp.float32)).astype(jnp.bfloat16)
    partial_out = jnp.einsum(
        "hce,hen->cn",
        gated,
        w_out.reshape(heads_here, head_dim, width),
        preferred_element_type=jnp.float32,
    )
    slice_width = width // n_head
    chunks = partial_out.reshape(row_count, n_head, slice_width).transpose(1, 0, 2)
    summed = ring_reduce_scatter(chunks, "head", n_head, head_index)
    residual = lax.dynamic_slice_in_dim(cand_wide, head_index * slice_width, slice_width, 1)
    row_ids = cand_index * row_count + jnp.arange(row_count, dtype=jnp.int32)
    count_mine = jnp.where(first_core, counts[0], counts[1])
    result = jnp.where((row_ids < count_mine)[:, None], residual + summed, 0.0).astype(jnp.bfloat16)
    result_other = lax.ppermute(result, "hist", swap(n_hist))
    first = jnp.where(first_core, result, result_other)
    second = jnp.where(first_core, result_other, result)
    return jnp.stack([first, second])


def solution(mesh):
    in_specs = (
        P("grp", "cand", None),
        P(None, None, "head"),
        P("head", None),
        P("grp", ("cand", "hist"), "head"),
        P("grp", ("cand", "hist"), "head"),
        P("grp"),
        P("grp"),
    )
    out_specs = P("grp", "cand", "head")
    return jax.shard_map(shards, mesh=mesh, in_specs=in_specs, out_specs=out_specs, check_vma=False)
```

```python
import functools
import math

import jax
import jax.numpy as jnp
from jax import lax
from jax.experimental import pallas as pl
from jax.experimental.pallas import tpu as pltpu
from jax.sharding import PartitionSpec as P

HEADS = 16
LANES = 128


def layer_norm_rows(values, width):
    row_mean = jnp.sum(values, axis=-1, keepdims=True) / width
    row_square = jnp.sum(values * values, axis=-1, keepdims=True) / width
    return (values - row_mean) * lax.rsqrt(row_square - row_mean * row_mean + 1e-05)


def ring(n):
    return [(i, (i + 1) % n) for i in range(n)]


def swap(n):
    return [(i, n - 1 - i) for i in range(n)]


def attend_kernel(limits, q_ref, k_ref, v_ref, o_ref, *, head_dim, row_tile, key_tile):
    kv = pl.program_id(0)
    rt = pl.program_id(1)
    rows_live = limits[0]
    keys_live = limits[1]
    rows = pl.ds(pl.multiple_of(rt * row_tile, row_tile), row_tile)
    width = q_ref.shape[1]
    half_scale = 0.5 / math.sqrt(head_dim)

    @pl.when(kv == 0)
    def _():
        o_ref[rows, :] = jnp.zeros((row_tile, width), jnp.float32)

    @pl.when((rt * row_tile < rows_live) & (kv * key_tile < keys_live))
    def _():
        lane = lax.broadcasted_iota(jnp.int32, (1, LANES), 1)
        column = kv * key_tile + lax.broadcasted_iota(jnp.int32, (1, key_tile), 1)
        valid = column < keys_live
        for p in range(width // LANES):
            lanes = slice(p * LANES, (p + 1) * LANES)
            q_pair = q_ref[:, lanes]
            k_pair = k_ref[:, lanes]
            v_pair = v_ref[:, lanes]
            out = jnp.zeros((row_tile, LANES), jnp.float32)
            for hh in range(LANES // head_dim):
                in_head = (lane >= hh * head_dim) & (lane < (hh + 1) * head_dim)
                q_head = jnp.where(in_head, q_pair, jnp.zeros_like(q_pair))
                scores = lax.dot_general(
                    q_head, k_pair, (((1,), (1,)), ((), ())), preferred_element_type=jnp.float32
                )
                halves = scores * half_scale
                weights = jnp.where(valid, halves + halves * jnp.tanh(halves), 0.0).astype(
                    jnp.bfloat16
                )
                v_head = jnp.where(in_head, v_pair, jnp.zeros_like(v_pair))
                out = out + jnp.dot(weights, v_head, preferred_element_type=jnp.float32)
            o_ref[rows, lanes] += out


def attend(query_rows, hist_keys, hist_values, request, rows_live, keys_live, head_dim):
    row_count, width = query_rows.shape
    key_count = hist_keys.shape[1]
    row_tile = min(128, row_count)
    key_tile = min(1024, key_count)
    key_tiles = key_count // key_tile
    last_tile = jnp.clip((keys_live + key_tile - 1) // key_tile - 1, 0, key_tiles - 1)
    limits = jnp.stack([rows_live, keys_live, request, last_tile]).astype(jnp.int32)
    kernel = functools.partial(
        attend_kernel, head_dim=head_dim, row_tile=row_tile, key_tile=key_tile
    )
    kv_spec = pl.BlockSpec(
        (None, key_tile, width), lambda kv, rt, lim: (lim[2], jnp.minimum(kv, lim[3]), 0)
    )
    flops = 4 * row_count * key_count * width
    return pl.pallas_call(
        kernel,
        out_shape=jax.ShapeDtypeStruct((row_count, width), jnp.float32),
        grid_spec=pltpu.PrefetchScalarGridSpec(
            num_scalar_prefetch=1,
            grid=(key_tiles, row_count // row_tile),
            in_specs=[
                pl.BlockSpec((row_tile, width), lambda kv, rt, lim: (rt, 0)),
                kv_spec,
                kv_spec,
            ],
            out_specs=pl.BlockSpec((row_count, width), lambda kv, rt, lim: (0, 0)),
        ),
        cost_estimate=pl.CostEstimate(
            flops=flops,
            transcendentals=row_count * key_count * (width // head_dim),
            bytes_accessed=2 * key_count * width * 2 + row_count * width * 6,
        ),
    )(limits, query_rows, hist_keys, hist_values)


def ring_reduce_scatter(chunks, axis, n, index):
    acc = None
    for t in range(1, n):
        part = lax.dynamic_index_in_dim(chunks, (index - t) % n, 0, keepdims=False)
        if acc is not None:
            part = part + acc.astype(jnp.float32)
        acc = lax.ppermute(part.astype(jnp.bfloat16), axis, ring(n))
    own = lax.dynamic_index_in_dim(chunks, index, 0, keepdims=False)
    return own if acc is None else own + acc.astype(jnp.float32)


def ring_sum(values, axis, n):
    total = values
    moving = values
    for _ in range(1, n):
        moving = lax.ppermute(moving, axis, ring(n))
        total = total + moving
    return total


def shards(candidates, w_in, w_out, hist_keys, hist_values, lengths, counts):
    requests, row_count, width = candidates.shape
    width_here = w_in.shape[2]
    head_dim = width // HEADS
    n_cand = lax.axis_size("cand")
    n_hist = lax.axis_size("hist")
    n_head = lax.axis_size("head")
    cand_index = lax.axis_index("cand")
    hist_index = lax.axis_index("hist")
    head_index = lax.axis_index("head")
    assert n_hist == 2 and requests == 2
    first_core = hist_index == 0
    mine = hist_index
    other = 1 - hist_index

    cand_mine = jnp.where(first_core, candidates[0], candidates[1])
    cand_wide = cand_mine.astype(jnp.float32)
    normed = layer_norm_rows(cand_wide, width).astype(jnp.bfloat16)
    projected = jnp.dot(
        normed, w_in.reshape(width, 2 * width_here), preferred_element_type=jnp.float32
    )
    activated = jax.nn.silu(projected).astype(jnp.bfloat16).reshape(row_count, 2, width_here)
    gate_u = activated[:, 0, :]
    query_mine = activated[:, 1, :]

    blocks = hist_keys.shape[1]
    key_base = (cand_index * n_hist + hist_index) * blocks
    length_mine = jnp.where(first_core, lengths[0], lengths[1])
    length_other = jnp.where(first_core, lengths[1], lengths[0])
    count_mine = jnp.where(first_core, counts[0], counts[1])
    count_other = jnp.where(first_core, counts[1], counts[0])
    keys_live_mine = jnp.clip(length_mine - key_base, 0, blocks)
    keys_live_other = jnp.clip(length_other - key_base, 0, blocks)

    query_k = query_mine
    own_sum = None
    acc = None
    for k in range(n_cand):
        if k > 0:
            query_k = lax.ppermute(query_k, "cand", ring(n_cand))
        row_base = ((cand_index - k) % n_cand) * row_count
        query_partner = lax.ppermute(query_k, "hist", swap(n_hist))
        part_other = attend(
            query_partner, hist_keys, hist_values, other,
            jnp.clip(count_other - row_base, 0, row_count), keys_live_other, head_dim,
        )
        part_mine = attend(
            query_k, hist_keys, hist_values, mine,
            jnp.clip(count_mine - row_base, 0, row_count), keys_live_mine, head_dim,
        )
        chip_sum = part_mine + lax.ppermute(part_other, "hist", swap(n_hist))
        if k == 0:
            own_sum = chip_sum
        else:
            if acc is not None:
                chip_sum = chip_sum + acc.astype(jnp.float32)
            acc = lax.ppermute(chip_sum.astype(jnp.bfloat16), "cand", ring(n_cand))
    total = own_sum if acc is None else own_sum + acc.astype(jnp.float32)

    attended = total / length_mine.astype(jnp.float32)
    moments = ring_sum(
        jnp.stack([jnp.sum(attended, axis=-1), jnp.sum(attended * attended, axis=-1)]),
        "head",
        n_head,
    )
    row_mean = moments[0][:, None] / width
    row_square = moments[1][:, None] / width
    normed_out = (attended - row_mean) * lax.rsqrt(row_square - row_mean * row_mean + 1e-05)
    gated = (normed_out * gate_u.astype(jnp.float32)).astype(jnp.bfloat16)
    partial_out = jnp.dot(gated, w_out, preferred_element_type=jnp.float32)
    slice_width = width // n_head
    chunks = partial_out.reshape(row_count, n_head, slice_width).transpose(1, 0, 2)
    summed = ring_reduce_scatter(chunks, "head", n_head, head_index)
    residual = lax.dynamic_slice_in_dim(cand_wide, head_index * slice_width, slice_width, 1)
    row_ids = cand_index * row_count + jnp.arange(row_count, dtype=jnp.int32)
    result = jnp.where((row_ids < count_mine)[:, None], residual + summed, 0.0).astype(jnp.bfloat16)
    result_other = lax.ppermute(result, "hist", swap(n_hist))
    first = jnp.where(first_core, result, result_other)
    second = jnp.where(first_core, result_other, result)
    return jnp.stack([first, second])


def solution(mesh):
    in_specs = (
        P("grp", "cand", None),
        P(None, None, "head"),
        P("head", None),
        P("grp", ("cand", "hist"), "head"),
        P("grp", ("cand", "hist"), "head"),
        P("grp"),
        P("grp"),
    )
    out_specs = P("grp", "cand", "head")
    return jax.shard_map(shards, mesh=mesh, in_specs=in_specs, out_specs=out_specs, check_vma=False)
```

```python
import functools
import math

import jax
import jax.numpy as jnp
from jax import lax
from jax.experimental import pallas as pl
from jax.experimental.pallas import tpu as pltpu
from jax.sharding import PartitionSpec as P

HEADS = 16
LANES = 128


def layer_norm_rows(values, width):
    row_mean = jnp.sum(values, axis=-1, keepdims=True) / width
    row_square = jnp.sum(values * values, axis=-1, keepdims=True) / width
    return (values - row_mean) * lax.rsqrt(row_square - row_mean * row_mean + 1e-05)


def ring(n):
    return [(i, (i + 1) % n) for i in range(n)]


def swap(n):
    return [(i, n - 1 - i) for i in range(n)]


def attend_kernel(limits, q_ref, kt_ref, v_ref, o_ref, *, offset, head_dim, row_tile, key_tile):
    kv = pl.program_id(0)
    rows_live = limits[offset]
    keys_live = limits[offset + 1]
    row_count, width = q_ref.shape
    half_scale = 0.5 / math.sqrt(head_dim)

    @pl.when(kv == 0)
    def _():
        o_ref[...] = jnp.zeros((row_count, width), jnp.float32)

    def compute(rows):
        lane = lax.broadcasted_iota(jnp.int32, (1, LANES), 1)
        column = kv * key_tile + lax.broadcasted_iota(jnp.int32, (1, key_tile), 1)
        valid = column < keys_live
        def pair(p, carry):
            lanes = pl.ds(pl.multiple_of(p * LANES, LANES), LANES)
            q_pair = q_ref[0:rows, lanes]
            kt_pair = kt_ref[lanes, :]
            v_pair = v_ref[:, lanes]
            out = jnp.zeros((rows, LANES), jnp.float32)
            for hh in range(LANES // head_dim):
                in_head = (lane >= hh * head_dim) & (lane < (hh + 1) * head_dim)
                q_head = jnp.where(in_head, q_pair, jnp.zeros_like(q_pair))
                scores = jnp.dot(q_head, kt_pair, preferred_element_type=jnp.float32)
                halves = scores * half_scale
                weights = jnp.where(valid, halves + halves * jnp.tanh(halves), 0.0).astype(
                    jnp.bfloat16
                )
                v_head = jnp.where(in_head, v_pair, jnp.zeros_like(v_pair))
                out = out + jnp.dot(weights, v_head, preferred_element_type=jnp.float32)
            o_ref[0:rows, lanes] += out
            return carry

        lax.fori_loop(0, width // LANES, pair, 0)

    live = kv * key_tile < keys_live
    if row_count > row_tile:
        pl.when(live & (rows_live > row_tile))(lambda: compute(row_count))
        pl.when(live & (rows_live > 0) & (rows_live <= row_tile))(lambda: compute(row_tile))
    else:
        pl.when(live & (rows_live > 0))(lambda: compute(row_count))


def attend(query_rows, keys_t, hist_values, table, offset, head_dim):
    row_count, width = query_rows.shape
    key_count = hist_values.shape[1]
    row_tile = min(128, row_count)
    key_tile = min(1024, key_count)
    key_tiles = key_count // key_tile
    kernel = functools.partial(
        attend_kernel, offset=offset, head_dim=head_dim, row_tile=row_tile, key_tile=key_tile
    )
    flops = 4 * row_count * key_count * width
    return pl.pallas_call(
        kernel,
        out_shape=jax.ShapeDtypeStruct((row_count, width), jnp.float32),
        grid_spec=pltpu.PrefetchScalarGridSpec(
            num_scalar_prefetch=1,
            grid=(key_tiles,),
            in_specs=[
                pl.BlockSpec((row_count, width), lambda kv, lim: (0, 0)),
                pl.BlockSpec(
                    (None, width, key_tile),
                    lambda kv, lim: (lim[offset + 2], 0, jnp.minimum(kv, lim[offset + 3])),
                ),
                pl.BlockSpec(
                    (None, key_tile, width),
                    lambda kv, lim: (lim[offset + 2], jnp.minimum(kv, lim[offset + 3]), 0),
                ),
            ],
            out_specs=pl.BlockSpec((row_count, width), lambda kv, lim: (0, 0)),
        ),
        cost_estimate=pl.CostEstimate(
            flops=flops,
            transcendentals=row_count * key_count * (width // head_dim),
            bytes_accessed=2 * key_count * width * 2 + row_count * width * 6,
        ),
    )(table, query_rows, keys_t, hist_values)


def ring_reduce_scatter(chunks, axis, n, index):
    acc = None
    for t in range(1, n):
        part = lax.dynamic_index_in_dim(chunks, (index - t) % n, 0, keepdims=False)
        if acc is not None:
            part = part + acc.astype(jnp.float32)
        acc = lax.ppermute(part.astype(jnp.bfloat16), axis, ring(n))
    own = lax.dynamic_index_in_dim(chunks, index, 0, keepdims=False)
    return own if acc is None else own + acc.astype(jnp.float32)


def ring_sum(values, axis, n):
    total = values
    moving = values
    for _ in range(1, n):
        moving = lax.ppermute(moving, axis, ring(n))
        total = total + moving
    return total


def shards(candidates, w_in, w_out, hist_keys, hist_values, lengths, counts):
    requests, row_count, width = candidates.shape
    width_here = w_in.shape[2]
    head_dim = width // HEADS
    n_cand = lax.axis_size("cand")
    n_hist = lax.axis_size("hist")
    n_head = lax.axis_size("head")
    cand_index = lax.axis_index("cand")
    hist_index = lax.axis_index("hist")
    head_index = lax.axis_index("head")
    assert n_hist == 2 and requests == 2
    first_core = hist_index == 0

    cand_mine = jnp.where(first_core, candidates[0], candidates[1])
    cand_wide = cand_mine.astype(jnp.float32)
    normed = layer_norm_rows(cand_wide, width).astype(jnp.bfloat16)
    projected = jnp.dot(
        normed, w_in.reshape(width, 2 * width_here), preferred_element_type=jnp.float32
    )
    activated = jax.nn.silu(projected).astype(jnp.bfloat16).reshape(row_count, 2, width_here)
    gate_u = activated[:, 0, :]
    query_mine = activated[:, 1, :]

    blocks = hist_keys.shape[1]
    key_base = (cand_index * n_hist + hist_index) * blocks
    length_mine = jnp.where(first_core, lengths[0], lengths[1])
    count_mine = jnp.where(first_core, counts[0], counts[1])
    key_tile = min(1024, blocks)
    key_tiles = blocks // key_tile
    request = jnp.stack([hist_index, 1 - hist_index]).astype(jnp.int32)
    counts_r = jnp.take(counts, request)
    keys_live = jnp.clip(jnp.take(lengths, request) - key_base, 0, blocks)
    last_tile = jnp.clip((keys_live + key_tile - 1) // key_tile - 1, 0, key_tiles - 1)
    row_base = ((cand_index - jnp.arange(n_cand)) % n_cand) * row_count
    rows_live = jnp.clip(counts_r[None, :] - row_base[:, None], 0, row_count)
    table = jnp.stack(
        [
            rows_live,
            jnp.broadcast_to(keys_live, rows_live.shape),
            jnp.broadcast_to(request, rows_live.shape),
            jnp.broadcast_to(last_tile, rows_live.shape),
        ],
        axis=-1,
    ).astype(jnp.int32).reshape(-1)
    keys_t = jnp.swapaxes(hist_keys, 1, 2)

    query_k = query_mine
    own_sum = None
    acc = None
    for k in range(n_cand):
        if k > 0:
            query_k = lax.ppermute(query_k, "cand", ring(n_cand))
        part_mine = attend(query_k, keys_t, hist_values, table, 8 * k, head_dim)
        query_partner = lax.ppermute(query_k, "hist", swap(n_hist))
        part_other = attend(query_partner, keys_t, hist_values, table, 8 * k + 4, head_dim)
        chip_sum = part_mine + lax.ppermute(part_other, "hist", swap(n_hist))
        if k == 0:
            own_sum = chip_sum
        else:
            if acc is not None:
                chip_sum = chip_sum + acc.astype(jnp.float32)
            acc = lax.ppermute(chip_sum.astype(jnp.bfloat16), "cand", ring(n_cand))
    total = own_sum if acc is None else own_sum + acc.astype(jnp.float32)

    attended = total / length_mine.astype(jnp.float32)
    moments = ring_sum(
        jnp.stack([jnp.sum(attended, axis=-1), jnp.sum(attended * attended, axis=-1)]),
        "head",
        n_head,
    )
    row_mean = moments[0][:, None] / width
    row_square = moments[1][:, None] / width
    normed_out = (attended - row_mean) * lax.rsqrt(row_square - row_mean * row_mean + 1e-05)
    gated = (normed_out * gate_u.astype(jnp.float32)).astype(jnp.bfloat16)
    partial_out = jnp.dot(gated, w_out, preferred_element_type=jnp.float32)
    slice_width = width // n_head
    chunks = partial_out.reshape(row_count, n_head, slice_width).transpose(1, 0, 2)
    summed = ring_reduce_scatter(chunks, "head", n_head, head_index)
    residual = lax.dynamic_slice_in_dim(cand_wide, head_index * slice_width, slice_width, 1)
    row_ids = cand_index * row_count + jnp.arange(row_count, dtype=jnp.int32)
    result = jnp.where((row_ids < count_mine)[:, None], residual + summed, 0.0).astype(jnp.bfloat16)
    result_other = lax.ppermute(result, "hist", swap(n_hist))
    first = jnp.where(first_core, result, result_other)
    second = jnp.where(first_core, result_other, result)
    return jnp.stack([first, second])


def solution(mesh):
    in_specs = (
        P("grp", "cand", None),
        P(None, None, "head"),
        P("head", None),
        P("grp", ("cand", "hist"), "head"),
        P("grp", ("cand", "hist"), "head"),
        P("grp"),
        P("grp"),
    )
    out_specs = P("grp", "cand", "head")
    return jax.shard_map(shards, mesh=mesh, in_specs=in_specs, out_specs=out_specs, check_vma=False)
```

```python
import functools
import math

import jax
import jax.numpy as jnp
from jax import lax
from jax.experimental import pallas as pl
from jax.experimental.pallas import tpu as pltpu
from jax.sharding import PartitionSpec as P

HEADS = 16
LANES = 128


def layer_norm_rows(values, width):
    row_mean = jnp.sum(values, axis=-1, keepdims=True) / width
    row_square = jnp.sum(values * values, axis=-1, keepdims=True) / width
    return (values - row_mean) * lax.rsqrt(row_square - row_mean * row_mean + 1e-05)


def ring(n):
    return [(i, (i + 1) % n) for i in range(n)]


def swap(n):
    return [(i, n - 1 - i) for i in range(n)]


def attend_kernel(limits, q_ref, k_ref, v_ref, o_ref, *, offset, head_dim, row_tile, key_tile):
    kv = pl.program_id(0)
    rows_live = limits[offset]
    keys_live = limits[offset + 1]
    row_count, width = q_ref.shape
    half_scale = 0.5 / math.sqrt(head_dim)

    @pl.when(kv == 0)
    def _():
        o_ref[...] = jnp.zeros((row_count, width), jnp.float32)

    def compute(rows):
        lane = lax.broadcasted_iota(jnp.int32, (1, LANES), 1)
        column = kv * key_tile + lax.broadcasted_iota(jnp.int32, (1, key_tile), 1)
        valid = column < keys_live
        def pair(p, carry):
            lanes = pl.ds(pl.multiple_of(p * LANES, LANES), LANES)
            q_pair = q_ref[0:rows, lanes]
            k_pair = k_ref[:, lanes]
            v_pair = v_ref[:, lanes]
            out = jnp.zeros((rows, LANES), jnp.float32)
            for hh in range(LANES // head_dim):
                in_head = (lane >= hh * head_dim) & (lane < (hh + 1) * head_dim)
                q_head = jnp.where(in_head, q_pair, jnp.zeros_like(q_pair))
                scores = lax.dot_general(
                    q_head, k_pair, (((1,), (1,)), ((), ())), preferred_element_type=jnp.float32
                )
                halves = scores * half_scale
                weights = jnp.where(valid, halves + halves * jnp.tanh(halves), 0.0).astype(
                    jnp.bfloat16
                )
                v_head = jnp.where(in_head, v_pair, jnp.zeros_like(v_pair))
                out = out + jnp.dot(weights, v_head, preferred_element_type=jnp.float32)
            o_ref[0:rows, lanes] += out
            return carry

        lax.fori_loop(0, width // LANES, pair, 0)

    live = kv * key_tile < keys_live
    if row_count > row_tile:
        pl.when(live & (rows_live > row_tile))(lambda: compute(row_count))
        pl.when(live & (rows_live > 0) & (rows_live <= row_tile))(lambda: compute(row_tile))
    else:
        pl.when(live & (rows_live > 0))(lambda: compute(row_count))


def attend(query_rows, hist_keys, hist_values, table, offset, head_dim):
    row_count, width = query_rows.shape
    key_count = hist_values.shape[1]
    row_tile = min(128, row_count)
    key_tile = min(1024, key_count)
    key_tiles = key_count // key_tile
    kernel = functools.partial(
        attend_kernel, offset=offset, head_dim=head_dim, row_tile=row_tile, key_tile=key_tile
    )
    flops = 4 * row_count * key_count * width
    return pl.pallas_call(
        kernel,
        out_shape=jax.ShapeDtypeStruct((row_count, width), jnp.float32),
        grid_spec=pltpu.PrefetchScalarGridSpec(
            num_scalar_prefetch=1,
            grid=(key_tiles,),
            in_specs=[
                pl.BlockSpec((row_count, width), lambda kv, lim: (0, 0)),
                pl.BlockSpec(
                    (None, key_tile, width),
                    lambda kv, lim: (lim[offset + 2], jnp.minimum(kv, lim[offset + 3]), 0),
                ),
                pl.BlockSpec(
                    (None, key_tile, width),
                    lambda kv, lim: (lim[offset + 2], jnp.minimum(kv, lim[offset + 3]), 0),
                ),
            ],
            out_specs=pl.BlockSpec((row_count, width), lambda kv, lim: (0, 0)),
        ),
        cost_estimate=pl.CostEstimate(
            flops=flops,
            transcendentals=row_count * key_count * (width // head_dim),
            bytes_accessed=2 * key_count * width * 2 + row_count * width * 6,
        ),
    )(table, query_rows, hist_keys, hist_values)


def ring_reduce_scatter(chunks, axis, n, index):
    acc = None
    for t in range(1, n):
        part = lax.dynamic_index_in_dim(chunks, (index - t) % n, 0, keepdims=False)
        if acc is not None:
            part = part + acc.astype(jnp.float32)
        acc = lax.ppermute(part.astype(jnp.bfloat16), axis, ring(n))
    own = lax.dynamic_index_in_dim(chunks, index, 0, keepdims=False)
    return own if acc is None else own + acc.astype(jnp.float32)


def ring_sum(values, axis, n):
    total = values
    moving = values
    for _ in range(1, n):
        moving = lax.ppermute(moving, axis, ring(n))
        total = total + moving
    return total


def shards(candidates, w_in, w_out, hist_keys, hist_values, lengths, counts):
    requests, row_count, width = candidates.shape
    width_here = w_in.shape[2]
    head_dim = width // HEADS
    n_cand = lax.axis_size("cand")
    n_hist = lax.axis_size("hist")
    n_head = lax.axis_size("head")
    cand_index = lax.axis_index("cand")
    hist_index = lax.axis_index("hist")
    head_index = lax.axis_index("head")
    assert n_hist == 2 and requests == 2
    first_core = hist_index == 0

    cand_wide_all = candidates.astype(jnp.float32)
    normed = layer_norm_rows(cand_wide_all, width).astype(jnp.bfloat16)
    projected = jnp.dot(
        normed.reshape(requests * row_count, width),
        w_in.reshape(width, 2 * width_here),
        preferred_element_type=jnp.float32,
    )
    activated = (
        jax.nn.silu(projected).astype(jnp.bfloat16).reshape(requests, row_count, 2, width_here)
    )
    cand_wide = jnp.where(first_core, cand_wide_all[0], cand_wide_all[1])
    gate_u = jnp.where(first_core, activated[0, :, 0, :], activated[1, :, 0, :])
    query_mine = jnp.where(first_core, activated[0, :, 1, :], activated[1, :, 1, :])
    query_other = jnp.where(first_core, activated[1, :, 1, :], activated[0, :, 1, :])

    blocks = hist_keys.shape[1]
    key_base = (cand_index * n_hist + hist_index) * blocks
    length_mine = jnp.where(first_core, lengths[0], lengths[1])
    count_mine = jnp.where(first_core, counts[0], counts[1])
    key_tile = min(1024, blocks)
    key_tiles = blocks // key_tile
    request = jnp.stack([hist_index, 1 - hist_index]).astype(jnp.int32)
    counts_r = jnp.take(counts, request)
    keys_live = jnp.clip(jnp.take(lengths, request) - key_base, 0, blocks)
    last_tile = jnp.clip((keys_live + key_tile - 1) // key_tile - 1, 0, key_tiles - 1)
    row_base = ((cand_index - jnp.arange(n_cand)) % n_cand) * row_count
    rows_live = jnp.clip(counts_r[None, :] - row_base[:, None], 0, row_count)
    table = jnp.stack(
        [
            rows_live,
            jnp.broadcast_to(keys_live, rows_live.shape),
            jnp.broadcast_to(request, rows_live.shape),
            jnp.broadcast_to(last_tile, rows_live.shape),
        ],
        axis=-1,
    ).astype(jnp.int32).reshape(-1)

    query_k = query_mine
    own_sum = None
    acc = None
    for k in range(n_cand):
        if k > 0:
            query_k = lax.ppermute(query_k, "cand", ring(n_cand))
        part_mine = attend(query_k, hist_keys, hist_values, table, 8 * k, head_dim)
        query_partner = query_other if k == 0 else lax.ppermute(query_k, "hist", swap(n_hist))
        part_other = attend(query_partner, hist_keys, hist_values, table, 8 * k + 4, head_dim)
        chip_sum = part_mine + lax.ppermute(part_other, "hist", swap(n_hist))
        if k == 0:
            own_sum = chip_sum
        else:
            if acc is not None:
                chip_sum = chip_sum + acc.astype(jnp.float32)
            acc = lax.ppermute(chip_sum.astype(jnp.bfloat16), "cand", ring(n_cand))
    total = own_sum if acc is None else own_sum + acc.astype(jnp.float32)

    attended = total / length_mine.astype(jnp.float32)
    moments = ring_sum(
        jnp.stack([jnp.sum(attended, axis=-1), jnp.sum(attended * attended, axis=-1)]),
        "head",
        n_head,
    )
    row_mean = moments[0][:, None] / width
    row_square = moments[1][:, None] / width
    normed_out = (attended - row_mean) * lax.rsqrt(row_square - row_mean * row_mean + 1e-05)
    gated = (normed_out * gate_u.astype(jnp.float32)).astype(jnp.bfloat16)
    partial_out = jnp.dot(gated, w_out, preferred_element_type=jnp.float32)
    slice_width = width // n_head
    chunks = partial_out.reshape(row_count, n_head, slice_width).transpose(1, 0, 2)
    summed = ring_reduce_scatter(chunks, "head", n_head, head_index)
    residual = lax.dynamic_slice_in_dim(cand_wide, head_index * slice_width, slice_width, 1)
    row_ids = cand_index * row_count + jnp.arange(row_count, dtype=jnp.int32)
    result = jnp.where((row_ids < count_mine)[:, None], residual + summed, 0.0).astype(jnp.bfloat16)
    result_other = lax.ppermute(result, "hist", swap(n_hist))
    first = jnp.where(first_core, result, result_other)
    second = jnp.where(first_core, result_other, result)
    return jnp.stack([first, second])


def solution(mesh):
    in_specs = (
        P("grp", "cand", None),
        P(None, None, "head"),
        P("head", None),
        P("grp", ("cand", "hist"), "head"),
        P("grp", ("cand", "hist"), "head"),
        P("grp"),
        P("grp"),
    )
    out_specs = P("grp", "cand", "head")
    return jax.shard_map(shards, mesh=mesh, in_specs=in_specs, out_specs=out_specs, check_vma=False)
```

```python
import functools
import math

import jax
import jax.numpy as jnp
from jax import lax
from jax.experimental import pallas as pl
from jax.experimental.pallas import tpu as pltpu
from jax.sharding import PartitionSpec as P

HEADS = 16
LANES = 128


def layer_norm_rows(values, width):
    row_mean = jnp.sum(values, axis=-1, keepdims=True) / width
    row_square = jnp.sum(values * values, axis=-1, keepdims=True) / width
    return (values - row_mean) * lax.rsqrt(row_square - row_mean * row_mean + 1e-05)


def ring(n):
    return [(i, (i + 1) % n) for i in range(n)]


def swap(n):
    return [(i, n - 1 - i) for i in range(n)]


def attend_kernel(limits, q_ref, k_ref, v_ref, o_ref, *, offset, head_dim, row_tile, key_tile):
    kv = pl.program_id(0)
    rows_live = limits[offset]
    keys_live = limits[offset + 1]
    row_count, width = q_ref.shape
    half_scale = 0.5 / math.sqrt(head_dim)

    @pl.when(kv == 0)
    def _():
        o_ref[...] = jnp.zeros((row_count, width), jnp.float32)

    def compute(rows):
        lane = lax.broadcasted_iota(jnp.int32, (1, LANES), 1)
        column = kv * key_tile + lax.broadcasted_iota(jnp.int32, (1, key_tile), 1)
        valid = column < keys_live
        def pair(p, carry):
            lanes = pl.ds(pl.multiple_of(p * LANES, LANES), LANES)
            q_pair = q_ref[0:rows, lanes]
            k_pair = k_ref[:, lanes]
            v_pair = v_ref[:, lanes]
            heads = LANES // head_dim
            head_of_lane = lane // head_dim
            q_stack = jnp.concatenate(
                [jnp.where(head_of_lane == hh, q_pair, jnp.zeros_like(q_pair)) for hh in range(heads)],
                axis=0,
            )
            scores = lax.dot_general(
                q_stack, k_pair, (((1,), (1,)), ((), ())), preferred_element_type=jnp.float32
            )
            halves = scores * half_scale
            weights = jnp.where(valid, halves + halves * jnp.tanh(halves), 0.0).astype(jnp.bfloat16)
            mixed = jnp.dot(weights, v_pair, preferred_element_type=jnp.float32)
            out = mixed[0:rows]
            for hh in range(1, heads):
                out = jnp.where(head_of_lane == hh, mixed[hh * rows:(hh + 1) * rows], out)
            o_ref[0:rows, lanes] += out
            return carry

        lax.fori_loop(0, width // LANES, pair, 0)

    live = kv * key_tile < keys_live
    if row_count > row_tile:
        pl.when(live & (rows_live > row_tile))(lambda: compute(row_count))
        pl.when(live & (rows_live > 0) & (rows_live <= row_tile))(lambda: compute(row_tile))
    else:
        pl.when(live & (rows_live > 0))(lambda: compute(row_count))


def attend(query_rows, hist_keys, hist_values, table, offset, head_dim):
    row_count, width = query_rows.shape
    key_count = hist_values.shape[1]
    row_tile = min(128, row_count)
    key_tile = min(1024, key_count)
    key_tiles = key_count // key_tile
    kernel = functools.partial(
        attend_kernel, offset=offset, head_dim=head_dim, row_tile=row_tile, key_tile=key_tile
    )
    flops = 4 * row_count * key_count * width
    return pl.pallas_call(
        kernel,
        out_shape=jax.ShapeDtypeStruct((row_count, width), jnp.float32),
        grid_spec=pltpu.PrefetchScalarGridSpec(
            num_scalar_prefetch=1,
            grid=(key_tiles,),
            in_specs=[
                pl.BlockSpec((row_count, width), lambda kv, lim: (0, 0)),
                pl.BlockSpec(
                    (None, key_tile, width),
                    lambda kv, lim: (lim[offset + 2], jnp.minimum(kv, lim[offset + 3]), 0),
                ),
                pl.BlockSpec(
                    (None, key_tile, width),
                    lambda kv, lim: (lim[offset + 2], jnp.minimum(kv, lim[offset + 3]), 0),
                ),
            ],
            out_specs=pl.BlockSpec((row_count, width), lambda kv, lim: (0, 0)),
        ),
        cost_estimate=pl.CostEstimate(
            flops=flops,
            transcendentals=row_count * key_count * (width // head_dim),
            bytes_accessed=2 * key_count * width * 2 + row_count * width * 6,
        ),
    )(table, query_rows, hist_keys, hist_values)


def ring_reduce_scatter(chunks, axis, n, index):
    acc = None
    for t in range(1, n):
        part = lax.dynamic_index_in_dim(chunks, (index - t) % n, 0, keepdims=False)
        if acc is not None:
            part = part + acc.astype(jnp.float32)
        acc = lax.ppermute(part.astype(jnp.bfloat16), axis, ring(n))
    own = lax.dynamic_index_in_dim(chunks, index, 0, keepdims=False)
    return own if acc is None else own + acc.astype(jnp.float32)


def ring_sum(values, axis, n):
    total = values
    moving = values
    for _ in range(1, n):
        moving = lax.ppermute(moving, axis, ring(n))
        total = total + moving
    return total


def shards(candidates, w_in, w_out, hist_keys, hist_values, lengths, counts):
    requests, row_count, width = candidates.shape
    width_here = w_in.shape[2]
    head_dim = width // HEADS
    n_cand = lax.axis_size("cand")
    n_hist = lax.axis_size("hist")
    n_head = lax.axis_size("head")
    cand_index = lax.axis_index("cand")
    hist_index = lax.axis_index("hist")
    head_index = lax.axis_index("head")
    assert n_hist == 2 and requests == 2
    first_core = hist_index == 0

    cand_mine = jnp.where(first_core, candidates[0], candidates[1])
    cand_wide = cand_mine.astype(jnp.float32)
    normed = layer_norm_rows(cand_wide, width).astype(jnp.bfloat16)
    projected = jnp.dot(
        normed, w_in.reshape(width, 2 * width_here), preferred_element_type=jnp.float32
    )
    activated = jax.nn.silu(projected).astype(jnp.bfloat16).reshape(row_count, 2, width_here)
    gate_u = activated[:, 0, :]
    query_mine = activated[:, 1, :]

    blocks = hist_keys.shape[1]
    key_base = (cand_index * n_hist + hist_index) * blocks
    length_mine = jnp.where(first_core, lengths[0], lengths[1])
    count_mine = jnp.where(first_core, counts[0], counts[1])
    key_tile = min(1024, blocks)
    key_tiles = blocks // key_tile
    request = jnp.stack([hist_index, 1 - hist_index]).astype(jnp.int32)
    counts_r = jnp.take(counts, request)
    keys_live = jnp.clip(jnp.take(lengths, request) - key_base, 0, blocks)
    last_tile = jnp.clip((keys_live + key_tile - 1) // key_tile - 1, 0, key_tiles - 1)
    row_base = ((cand_index - jnp.arange(n_cand)) % n_cand) * row_count
    rows_live = jnp.clip(counts_r[None, :] - row_base[:, None], 0, row_count)
    table = jnp.stack(
        [
            rows_live,
            jnp.broadcast_to(keys_live, rows_live.shape),
            jnp.broadcast_to(request, rows_live.shape),
            jnp.broadcast_to(last_tile, rows_live.shape),
        ],
        axis=-1,
    ).astype(jnp.int32).reshape(-1)

    query_k = query_mine
    own_sum = None
    acc = None
    for k in range(n_cand):
        if k > 0:
            query_k = lax.ppermute(query_k, "cand", ring(n_cand))
        part_mine = attend(query_k, hist_keys, hist_values, table, 8 * k, head_dim)
        query_partner = lax.ppermute(query_k, "hist", swap(n_hist))
        part_other = attend(query_partner, hist_keys, hist_values, table, 8 * k + 4, head_dim)
        chip_sum = part_mine + lax.ppermute(part_other, "hist", swap(n_hist))
        if k == 0:
            own_sum = chip_sum
        else:
            if acc is not None:
                chip_sum = chip_sum + acc.astype(jnp.float32)
            acc = lax.ppermute(chip_sum.astype(jnp.bfloat16), "cand", ring(n_cand))
    total = own_sum if acc is None else own_sum + acc.astype(jnp.float32)

    attended = total / length_mine.astype(jnp.float32)
    moments = ring_sum(
        jnp.stack([jnp.sum(attended, axis=-1), jnp.sum(attended * attended, axis=-1)]),
        "head",
        n_head,
    )
    row_mean = moments[0][:, None] / width
    row_square = moments[1][:, None] / width
    normed_out = (attended - row_mean) * lax.rsqrt(row_square - row_mean * row_mean + 1e-05)
    gated = (normed_out * gate_u.astype(jnp.float32)).astype(jnp.bfloat16)
    partial_out = jnp.dot(gated, w_out, preferred_element_type=jnp.float32)
    slice_width = width // n_head
    chunks = partial_out.reshape(row_count, n_head, slice_width).transpose(1, 0, 2)
    summed = ring_reduce_scatter(chunks, "head", n_head, head_index)
    residual = lax.dynamic_slice_in_dim(cand_wide, head_index * slice_width, slice_width, 1)
    row_ids = cand_index * row_count + jnp.arange(row_count, dtype=jnp.int32)
    result = jnp.where((row_ids < count_mine)[:, None], residual + summed, 0.0).astype(jnp.bfloat16)
    result_other = lax.ppermute(result, "hist", swap(n_hist))
    first = jnp.where(first_core, result, result_other)
    second = jnp.where(first_core, result_other, result)
    return jnp.stack([first, second])


def solution(mesh):
    in_specs = (
        P("grp", "cand", None),
        P(None, None, "head"),
        P("head", None),
        P("grp", ("cand", "hist"), "head"),
        P("grp", ("cand", "hist"), "head"),
        P("grp"),
        P("grp"),
    )
    out_specs = P("grp", "cand", "head")
    return jax.shard_map(shards, mesh=mesh, in_specs=in_specs, out_specs=out_specs, check_vma=False)
```

```python
import functools
import math

import jax
import jax.numpy as jnp
from jax import lax
from jax.experimental import pallas as pl
from jax.experimental.pallas import tpu as pltpu
from jax.sharding import PartitionSpec as P

HEADS = 16
LANES = 128


def layer_norm_rows(values, width):
    row_mean = jnp.sum(values, axis=-1, keepdims=True) / width
    row_square = jnp.sum(values * values, axis=-1, keepdims=True) / width
    return (values - row_mean) * lax.rsqrt(row_square - row_mean * row_mean + 1e-05)


def ring(n):
    return [(i, (i + 1) % n) for i in range(n)]


def swap(n):
    return [(i, n - 1 - i) for i in range(n)]


def attend_kernel(limits, qa_ref, qb_ref, k_ref, v_ref, oa_ref, ob_ref, *, offset, head_dim,
                  row_tile, key_tile):
    r = pl.program_id(0)
    kv = pl.program_id(1)
    row_count, width = qa_ref.shape
    half_scale = 0.5 / math.sqrt(head_dim)

    def compute(q_ref, o_ref, rows, keys_live):
        lane = lax.broadcasted_iota(jnp.int32, (1, LANES), 1)
        column = kv * key_tile + lax.broadcasted_iota(jnp.int32, (1, key_tile), 1)
        valid = column < keys_live

        def pair(p, carry):
            lanes = pl.ds(pl.multiple_of(p * LANES, LANES), LANES)
            q_pair = q_ref[0:rows, lanes]
            k_pair = k_ref[:, lanes]
            v_pair = v_ref[:, lanes]
            heads = LANES // head_dim
            head_of_lane = lane // head_dim
            q_stack = jnp.concatenate(
                [jnp.where(head_of_lane == hh, q_pair, jnp.zeros_like(q_pair)) for hh in range(heads)],
                axis=0,
            )
            scores = lax.dot_general(
                q_stack, k_pair, (((1,), (1,)), ((), ())), preferred_element_type=jnp.float32
            )
            halves = scores * half_scale
            weights = jnp.where(valid, halves + halves * jnp.tanh(halves), 0.0).astype(jnp.bfloat16)
            mixed = jnp.dot(weights, v_pair, preferred_element_type=jnp.float32)
            out = mixed[0:rows]
            for hh in range(1, heads):
                out = jnp.where(head_of_lane == hh, mixed[hh * rows:(hh + 1) * rows], out)
            o_ref[0:rows, lanes] += out
            return carry

        lax.fori_loop(0, width // LANES, pair, 0)

    def request(which, q_ref, o_ref):
        rows_live = limits[offset + 4 * which]
        keys_live = limits[offset + 4 * which + 1]

        @pl.when((r == 0) & (kv == 0))
        def _():
            o_ref[...] = jnp.zeros((row_count, width), jnp.float32)

        live = (r == which) & (kv * key_tile < keys_live)
        if row_count > row_tile:
            pl.when(live & (rows_live > row_tile))(
                lambda: compute(q_ref, o_ref, row_count, keys_live)
            )
            pl.when(live & (rows_live > 0) & (rows_live <= row_tile))(
                lambda: compute(q_ref, o_ref, row_tile, keys_live)
            )
        else:
            pl.when(live & (rows_live > 0))(lambda: compute(q_ref, o_ref, row_count, keys_live))

    request(0, qa_ref, oa_ref)
    request(1, qb_ref, ob_ref)


def attend(query_a, query_b, hist_keys, hist_values, table, offset, head_dim):
    row_count, width = query_a.shape
    key_count = hist_values.shape[1]
    row_tile = min(128, row_count)
    key_tile = min(1024, key_count)
    key_tiles = key_count // key_tile
    kernel = functools.partial(
        attend_kernel, offset=offset, head_dim=head_dim, row_tile=row_tile, key_tile=key_tile
    )

    def kv_index(r, kv, lim):
        return (lim[offset + 4 * r + 2], jnp.minimum(kv, lim[offset + 4 * r + 3]), 0)

    flops = 8 * row_count * key_count * width
    out = jax.ShapeDtypeStruct((row_count, width), jnp.float32)
    whole = pl.BlockSpec((row_count, width), lambda r, kv, lim: (0, 0))
    return pl.pallas_call(
        kernel,
        out_shape=(out, out),
        grid_spec=pltpu.PrefetchScalarGridSpec(
            num_scalar_prefetch=1,
            grid=(2, key_tiles),
            in_specs=[
                whole,
                whole,
                pl.BlockSpec((None, key_tile, width), kv_index),
                pl.BlockSpec((None, key_tile, width), kv_index),
            ],
            out_specs=(whole, whole),
        ),
        cost_estimate=pl.CostEstimate(
            flops=flops,
            transcendentals=2 * row_count * key_count * (width // head_dim),
            bytes_accessed=4 * key_count * width * 2 + row_count * width * 12,
        ),
    )(table, query_a, query_b, hist_keys, hist_values)


def ring_reduce_scatter(chunks, axis, n, index):
    acc = None
    for t in range(1, n):
        part = lax.dynamic_index_in_dim(chunks, (index - t) % n, 0, keepdims=False)
        if acc is not None:
            part = part + acc.astype(jnp.float32)
        acc = lax.ppermute(part.astype(jnp.bfloat16), axis, ring(n))
    own = lax.dynamic_index_in_dim(chunks, index, 0, keepdims=False)
    return own if acc is None else own + acc.astype(jnp.float32)


def ring_sum(values, axis, n):
    total = values
    moving = values
    for _ in range(1, n):
        moving = lax.ppermute(moving, axis, ring(n))
        total = total + moving
    return total


def shards(candidates, w_in, w_out, hist_keys, hist_values, lengths, counts):
    requests, row_count, width = candidates.shape
    width_here = w_in.shape[2]
    head_dim = width // HEADS
    n_cand = lax.axis_size("cand")
    n_hist = lax.axis_size("hist")
    n_head = lax.axis_size("head")
    cand_index = lax.axis_index("cand")
    hist_index = lax.axis_index("hist")
    head_index = lax.axis_index("head")
    assert n_hist == 2 and requests == 2
    first_core = hist_index == 0

    cand_mine = jnp.where(first_core, candidates[0], candidates[1])
    cand_wide = cand_mine.astype(jnp.float32)
    normed = layer_norm_rows(cand_wide, width).astype(jnp.bfloat16)
    projected = jnp.dot(
        normed, w_in.reshape(width, 2 * width_here), preferred_element_type=jnp.float32
    )
    activated = jax.nn.silu(projected).astype(jnp.bfloat16).reshape(row_count, 2, width_here)
    gate_u = activated[:, 0, :]
    query_mine = activated[:, 1, :]

    blocks = hist_keys.shape[1]
    key_base = (cand_index * n_hist + hist_index) * blocks
    length_mine = jnp.where(first_core, lengths[0], lengths[1])
    count_mine = jnp.where(first_core, counts[0], counts[1])
    key_tile = min(1024, blocks)
    key_tiles = blocks // key_tile
    request = jnp.stack([hist_index, 1 - hist_index]).astype(jnp.int32)
    counts_r = jnp.take(counts, request)
    keys_live = jnp.clip(jnp.take(lengths, request) - key_base, 0, blocks)
    last_tile = jnp.clip((keys_live + key_tile - 1) // key_tile - 1, 0, key_tiles - 1)
    row_base = ((cand_index - jnp.arange(n_cand)) % n_cand) * row_count
    rows_live = jnp.clip(counts_r[None, :] - row_base[:, None], 0, row_count)
    table = jnp.stack(
        [
            rows_live,
            jnp.broadcast_to(keys_live, rows_live.shape),
            jnp.broadcast_to(request, rows_live.shape),
            jnp.broadcast_to(last_tile, rows_live.shape),
        ],
        axis=-1,
    ).astype(jnp.int32).reshape(-1)

    query_k = query_mine
    own_sum = None
    acc = None
    for k in range(n_cand):
        if k > 0:
            query_k = lax.ppermute(query_k, "cand", ring(n_cand))
        query_partner = lax.ppermute(query_k, "hist", swap(n_hist))
        part_mine, part_other = attend(
            query_k, query_partner, hist_keys, hist_values, table, 8 * k, head_dim
        )
        chip_sum = part_mine + lax.ppermute(part_other, "hist", swap(n_hist))
        if k == 0:
            own_sum = chip_sum
        else:
            if acc is not None:
                chip_sum = chip_sum + acc.astype(jnp.float32)
            acc = lax.ppermute(chip_sum.astype(jnp.bfloat16), "cand", ring(n_cand))
    total = own_sum if acc is None else own_sum + acc.astype(jnp.float32)

    attended = total / length_mine.astype(jnp.float32)
    moments = ring_sum(
        jnp.stack([jnp.sum(attended, axis=-1), jnp.sum(attended * attended, axis=-1)]),
        "head",
        n_head,
    )
    row_mean = moments[0][:, None] / width
    row_square = moments[1][:, None] / width
    normed_out = (attended - row_mean) * lax.rsqrt(row_square - row_mean * row_mean + 1e-05)
    gated = (normed_out * gate_u.astype(jnp.float32)).astype(jnp.bfloat16)
    partial_out = jnp.dot(gated, w_out, preferred_element_type=jnp.float32)
    slice_width = width // n_head
    chunks = partial_out.reshape(row_count, n_head, slice_width).transpose(1, 0, 2)
    summed = ring_reduce_scatter(chunks, "head", n_head, head_index)
    residual = lax.dynamic_slice_in_dim(cand_wide, head_index * slice_width, slice_width, 1)
    row_ids = cand_index * row_count + jnp.arange(row_count, dtype=jnp.int32)
    result = jnp.where((row_ids < count_mine)[:, None], residual + summed, 0.0).astype(jnp.bfloat16)
    result_other = lax.ppermute(result, "hist", swap(n_hist))
    first = jnp.where(first_core, result, result_other)
    second = jnp.where(first_core, result_other, result)
    return jnp.stack([first, second])


def solution(mesh):
    in_specs = (
        P("grp", "cand", None),
        P(None, None, "head"),
        P("head", None),
        P("grp", ("cand", "hist"), "head"),
        P("grp", ("cand", "hist"), "head"),
        P("grp"),
        P("grp"),
    )
    out_specs = P("grp", "cand", "head")
    return jax.shard_map(shards, mesh=mesh, in_specs=in_specs, out_specs=out_specs, check_vma=False)
```

```python
import functools
import math

import jax
import jax.numpy as jnp
from jax import lax
from jax.experimental import pallas as pl
from jax.experimental.pallas import tpu as pltpu
from jax.sharding import PartitionSpec as P

HEADS = 16
LANES = 128


def layer_norm_rows(values, width):
    row_mean = jnp.sum(values, axis=-1, keepdims=True) / width
    row_square = jnp.sum(values * values, axis=-1, keepdims=True) / width
    return (values - row_mean) * lax.rsqrt(row_square - row_mean * row_mean + 1e-05)


def ring(n):
    return [(i, (i + 1) % n) for i in range(n)]


def swap(n):
    return [(i, n - 1 - i) for i in range(n)]


def attend_kernel(limits, qa_ref, qb_ref, k_ref, v_ref, oa_ref, ob_ref, *, offset, head_dim,
                  row_tile, key_tile):
    r = pl.program_id(0)
    kv = pl.program_id(1)
    row_count, width = qa_ref.shape
    half_scale = 0.5 / math.sqrt(head_dim)

    def compute(q_ref, o_ref, rows, keys_live):
        lane = lax.broadcasted_iota(jnp.int32, (1, LANES), 1)
        column = kv * key_tile + lax.broadcasted_iota(jnp.int32, (1, key_tile), 1)
        valid = column < keys_live

        def pair(p, carry):
            lanes = pl.ds(pl.multiple_of(p * LANES, LANES), LANES)
            q_pair = q_ref[0:rows, lanes]
            k_pair = k_ref[:, lanes]
            v_pair = v_ref[:, lanes]
            heads = LANES // head_dim
            head_of_lane = lane // head_dim
            q_stack = jnp.concatenate(
                [jnp.where(head_of_lane == hh, q_pair, jnp.zeros_like(q_pair)) for hh in range(heads)],
                axis=0,
            )
            scores = lax.dot_general(
                q_stack, k_pair, (((1,), (1,)), ((), ())), preferred_element_type=jnp.float32
            )
            halves = scores * half_scale
            weights = jnp.where(valid, halves + halves * jnp.tanh(halves), 0.0).astype(jnp.bfloat16)
            mixed = jnp.dot(weights, v_pair, preferred_element_type=jnp.float32)
            out = mixed[0:rows]
            for hh in range(1, heads):
                out = jnp.where(head_of_lane == hh, mixed[hh * rows:(hh + 1) * rows], out)
            o_ref[0:rows, lanes] += out
            return carry

        lax.fori_loop(0, width // LANES, pair, 0)

    def request(which, q_ref, o_ref):
        rows_live = limits[offset + 4 * which]
        keys_live = limits[offset + 4 * which + 1]

        @pl.when((r == 0) & (kv == 0))
        def _():
            o_ref[...] = jnp.zeros((row_count, width), jnp.float32)

        live = (r == which) & (kv * key_tile < keys_live)
        if row_count > row_tile:
            pl.when(live & (rows_live > row_tile))(
                lambda: compute(q_ref, o_ref, row_count, keys_live)
            )
            pl.when(live & (rows_live > 0) & (rows_live <= row_tile))(
                lambda: compute(q_ref, o_ref, row_tile, keys_live)
            )
        else:
            pl.when(live & (rows_live > 0))(lambda: compute(q_ref, o_ref, row_count, keys_live))

    request(0, qa_ref, oa_ref)
    request(1, qb_ref, ob_ref)


def attend(query_a, query_b, hist_keys, hist_values, table, offset, head_dim):
    row_count, width = query_a.shape
    key_count = hist_values.shape[1]
    row_tile = min(128, row_count)
    key_tile = min(1024, key_count)
    key_tiles = key_count // key_tile
    kernel = functools.partial(
        attend_kernel, offset=offset, head_dim=head_dim, row_tile=row_tile, key_tile=key_tile
    )

    def kv_index(r, kv, lim):
        return (lim[offset + 4 * r + 2], jnp.minimum(kv, lim[offset + 4 * r + 3]), 0)

    flops = 8 * row_count * key_count * width
    out = jax.ShapeDtypeStruct((row_count, width), jnp.float32)
    whole = pl.BlockSpec((row_count, width), lambda r, kv, lim: (0, 0))
    return pl.pallas_call(
        kernel,
        out_shape=(out, out),
        grid_spec=pltpu.PrefetchScalarGridSpec(
            num_scalar_prefetch=1,
            grid=(2, key_tiles),
            in_specs=[
                whole,
                whole,
                pl.BlockSpec((None, key_tile, width), kv_index),
                pl.BlockSpec((None, key_tile, width), kv_index),
            ],
            out_specs=(whole, whole),
        ),
        cost_estimate=pl.CostEstimate(
            flops=flops,
            transcendentals=2 * row_count * key_count * (width // head_dim),
            bytes_accessed=4 * key_count * width * 2 + row_count * width * 12,
        ),
    )(table, query_a, query_b, hist_keys, hist_values)


def ring_reduce_scatter(chunks, axis, n, index):
    acc = None
    for t in range(1, n):
        part = lax.dynamic_index_in_dim(chunks, (index - t) % n, 0, keepdims=False)
        if acc is not None:
            part = part + acc.astype(jnp.float32)
        acc = lax.ppermute(part.astype(jnp.bfloat16), axis, ring(n))
    own = lax.dynamic_index_in_dim(chunks, index, 0, keepdims=False)
    return own if acc is None else own + acc.astype(jnp.float32)


def ring_sum(values, axis, n):
    total = values
    moving = values
    for _ in range(1, n):
        moving = lax.ppermute(moving, axis, ring(n))
        total = total + moving
    return total


def shards(candidates, w_in, w_out, hist_keys, hist_values, lengths, counts):
    requests, row_count, width = candidates.shape
    width_here = w_in.shape[2]
    head_dim = width // HEADS
    n_cand = lax.axis_size("cand")
    n_hist = lax.axis_size("hist")
    n_head = lax.axis_size("head")
    cand_index = lax.axis_index("cand")
    hist_index = lax.axis_index("hist")
    head_index = lax.axis_index("head")
    assert n_hist == 2 and requests == 2
    first_core = hist_index == 0

    cand_mine = jnp.where(first_core, candidates[0], candidates[1])
    cand_wide = cand_mine.astype(jnp.float32)
    normed = layer_norm_rows(cand_wide, width).astype(jnp.bfloat16)
    projected = jnp.dot(
        normed, w_in.reshape(width, 2 * width_here), preferred_element_type=jnp.float32
    )
    activated = jax.nn.silu(projected).astype(jnp.bfloat16).reshape(row_count, 2, width_here)
    gate_u = activated[:, 0, :]
    query_mine = activated[:, 1, :]

    blocks = hist_keys.shape[1]
    key_base = (cand_index * n_hist + hist_index) * blocks
    length_mine = jnp.where(first_core, lengths[0], lengths[1])
    count_mine = jnp.where(first_core, counts[0], counts[1])
    key_tile = min(1024, blocks)
    key_tiles = blocks // key_tile
    request = jnp.stack([hist_index, 1 - hist_index]).astype(jnp.int32)
    counts_r = jnp.take(counts, request)
    keys_live = jnp.clip(jnp.take(lengths, request) - key_base, 0, blocks)
    last_tile = jnp.clip((keys_live + key_tile - 1) // key_tile - 1, 0, key_tiles - 1)
    row_base = ((cand_index - jnp.arange(n_cand)) % n_cand) * row_count
    rows_live = jnp.clip(counts_r[None, :] - row_base[:, None], 0, row_count)
    table = jnp.stack(
        [
            rows_live,
            jnp.broadcast_to(keys_live, rows_live.shape),
            jnp.broadcast_to(request, rows_live.shape),
            jnp.broadcast_to(last_tile, rows_live.shape),
        ],
        axis=-1,
    ).astype(jnp.int32).reshape(-1)

    query_k = query_mine
    own_sum = None
    acc = None
    forward = query_k
    previous = None
    for k in range(n_cand):
        if k > 0:
            query_k = lax.ppermute(forward, "cand", ring(n_cand))
            forward, _ = lax.optimization_barrier((query_k, previous))
        query_partner = lax.ppermute(forward, "hist", swap(n_hist))
        part_mine, part_other = attend(
            query_k, query_partner, hist_keys, hist_values, table, 8 * k, head_dim
        )
        previous = part_mine
        chip_sum = part_mine + lax.ppermute(part_other, "hist", swap(n_hist))
        if k == 0:
            own_sum = chip_sum
        else:
            if acc is not None:
                chip_sum = chip_sum + acc.astype(jnp.float32)
            acc = lax.ppermute(chip_sum.astype(jnp.bfloat16), "cand", ring(n_cand))
    total = own_sum if acc is None else own_sum + acc.astype(jnp.float32)

    attended = total / length_mine.astype(jnp.float32)
    moments = ring_sum(
        jnp.stack([jnp.sum(attended, axis=-1), jnp.sum(attended * attended, axis=-1)]),
        "head",
        n_head,
    )
    row_mean = moments[0][:, None] / width
    row_square = moments[1][:, None] / width
    normed_out = (attended - row_mean) * lax.rsqrt(row_square - row_mean * row_mean + 1e-05)
    gated = (normed_out * gate_u.astype(jnp.float32)).astype(jnp.bfloat16)
    partial_out = jnp.dot(gated, w_out, preferred_element_type=jnp.float32)
    slice_width = width // n_head
    chunks = partial_out.reshape(row_count, n_head, slice_width).transpose(1, 0, 2)
    summed = ring_reduce_scatter(chunks, "head", n_head, head_index)
    residual = lax.dynamic_slice_in_dim(cand_wide, head_index * slice_width, slice_width, 1)
    row_ids = cand_index * row_count + jnp.arange(row_count, dtype=jnp.int32)
    result = jnp.where((row_ids < count_mine)[:, None], residual + summed, 0.0).astype(jnp.bfloat16)
    result_other = lax.ppermute(result, "hist", swap(n_hist))
    first = jnp.where(first_core, result, result_other)
    second = jnp.where(first_core, result_other, result)
    return jnp.stack([first, second])


def solution(mesh):
    in_specs = (
        P("grp", "cand", None),
        P(None, None, "head"),
        P("head", None),
        P("grp", ("cand", "hist"), "head"),
        P("grp", ("cand", "hist"), "head"),
        P("grp"),
        P("grp"),
    )
    out_specs = P("grp", "cand", "head")
    return jax.shard_map(shards, mesh=mesh, in_specs=in_specs, out_specs=out_specs, check_vma=False)
```

```python
import functools
import math

import jax
import jax.numpy as jnp
from jax import lax
from jax.experimental import pallas as pl
from jax.experimental.pallas import tpu as pltpu
from jax.sharding import PartitionSpec as P

HEADS = 16
LANES = 128


def layer_norm_rows(values, width):
    row_mean = jnp.sum(values, axis=-1, keepdims=True) / width
    row_square = jnp.sum(values * values, axis=-1, keepdims=True) / width
    return (values - row_mean) * lax.rsqrt(row_square - row_mean * row_mean + 1e-05)


def ring(n):
    return [(i, (i + 1) % n) for i in range(n)]


def swap(n):
    return [(i, n - 1 - i) for i in range(n)]


def attend_kernel(limits, qa_ref, qb_ref, k_ref, v_ref, oa_ref, ob_ref, *, offset, head_dim,
                  row_tile, key_tile):
    r = pl.program_id(0)
    kv = pl.program_id(1)
    row_count, width = qa_ref.shape
    half_scale = 0.5 / math.sqrt(head_dim)

    def compute(q_ref, o_ref, rows, keys_live):
        lane = lax.broadcasted_iota(jnp.int32, (1, LANES), 1)
        column = kv * key_tile + lax.broadcasted_iota(jnp.int32, (1, key_tile), 1)
        valid = column < keys_live

        def pair(p, carry):
            lanes = pl.ds(pl.multiple_of(p * LANES, LANES), LANES)
            q_pair = q_ref[0:rows, lanes]
            k_pair = k_ref[:, lanes]
            v_pair = v_ref[:, lanes]
            heads = LANES // head_dim
            head_of_lane = lane // head_dim
            q_stack = jnp.concatenate(
                [jnp.where(head_of_lane == hh, q_pair, jnp.zeros_like(q_pair)) for hh in range(heads)],
                axis=0,
            )
            scores = lax.dot_general(
                q_stack, k_pair, (((1,), (1,)), ((), ())), preferred_element_type=jnp.float32
            )
            halves = scores * half_scale
            weights = jnp.where(valid, halves + halves * jnp.tanh(halves), 0.0).astype(jnp.bfloat16)
            mixed = jnp.dot(weights, v_pair, preferred_element_type=jnp.float32)
            out = mixed[0:rows]
            for hh in range(1, heads):
                out = jnp.where(head_of_lane == hh, mixed[hh * rows:(hh + 1) * rows], out)
            o_ref[0:rows, lanes] += out
            return carry

        lax.fori_loop(0, width // LANES, pair, 0)

    def request(which, q_ref, o_ref):
        rows_live = limits[offset + 4 * which]
        keys_live = limits[offset + 4 * which + 1]

        @pl.when((r == 0) & (kv == 0))
        def _():
            o_ref[...] = jnp.zeros((row_count, width), jnp.float32)

        live = (r == which) & (kv * key_tile < keys_live)
        if row_count > row_tile:
            pl.when(live & (rows_live > row_tile))(
                lambda: compute(q_ref, o_ref, row_count, keys_live)
            )
            pl.when(live & (rows_live > 0) & (rows_live <= row_tile))(
                lambda: compute(q_ref, o_ref, row_tile, keys_live)
            )
        else:
            pl.when(live & (rows_live > 0))(lambda: compute(q_ref, o_ref, row_count, keys_live))

    request(0, qa_ref, oa_ref)
    request(1, qb_ref, ob_ref)


def attend(query_a, query_b, hist_keys, hist_values, table, offset, head_dim):
    row_count, width = query_a.shape
    key_count = hist_values.shape[1]
    row_tile = min(128, row_count)
    key_tile = min(1024, key_count)
    key_tiles = key_count // key_tile
    kernel = functools.partial(
        attend_kernel, offset=offset, head_dim=head_dim, row_tile=row_tile, key_tile=key_tile
    )

    def kv_index(r, kv, lim):
        return (lim[offset + 4 * r + 2], jnp.minimum(kv, lim[offset + 4 * r + 3]), 0)

    flops = 8 * row_count * key_count * width
    out = jax.ShapeDtypeStruct((row_count, width), jnp.float32)
    whole = pl.BlockSpec((row_count, width), lambda r, kv, lim: (0, 0))
    return pl.pallas_call(
        kernel,
        out_shape=(out, out),
        grid_spec=pltpu.PrefetchScalarGridSpec(
            num_scalar_prefetch=1,
            grid=(2, key_tiles),
            in_specs=[
                whole,
                whole,
                pl.BlockSpec((None, key_tile, width), kv_index),
                pl.BlockSpec((None, key_tile, width), kv_index),
            ],
            out_specs=(whole, whole),
        ),
        cost_estimate=pl.CostEstimate(
            flops=flops,
            transcendentals=2 * row_count * key_count * (width // head_dim),
            bytes_accessed=4 * key_count * width * 2 + row_count * width * 12,
        ),
    )(table, query_a, query_b, hist_keys, hist_values)


def ring_reduce_scatter(chunks, axis, n, index):
    acc = None
    for t in range(1, n):
        part = lax.dynamic_index_in_dim(chunks, (index - t) % n, 0, keepdims=False)
        if acc is not None:
            part = part + acc.astype(jnp.float32)
        acc = lax.ppermute(part.astype(jnp.bfloat16), axis, ring(n))
    own = lax.dynamic_index_in_dim(chunks, index, 0, keepdims=False)
    return own if acc is None else own + acc.astype(jnp.float32)


def ring_sum(values, axis, n):
    total = values
    moving = values
    for _ in range(1, n):
        moving = lax.ppermute(moving, axis, ring(n))
        total = total + moving
    return total


def shards(candidates, w_in, w_out, hist_keys, hist_values, lengths, counts):
    requests, row_count, width = candidates.shape
    width_here = w_in.shape[2]
    head_dim = width // HEADS
    n_cand = lax.axis_size("cand")
    n_hist = lax.axis_size("hist")
    n_head = lax.axis_size("head")
    cand_index = lax.axis_index("cand")
    hist_index = lax.axis_index("hist")
    head_index = lax.axis_index("head")
    assert n_hist == 2 and requests == 2
    first_core = hist_index == 0

    cand_mine = jnp.where(first_core, candidates[0], candidates[1])
    cand_wide = cand_mine.astype(jnp.float32)
    normed = layer_norm_rows(cand_wide, width).astype(jnp.bfloat16)
    projected = jnp.dot(
        normed, w_in.reshape(width, 2 * width_here), preferred_element_type=jnp.float32
    )
    activated = jax.nn.silu(projected).astype(jnp.bfloat16).reshape(row_count, 2, width_here)
    gate_u = activated[:, 0, :]
    query_mine = activated[:, 1, :]

    blocks = hist_keys.shape[1]
    key_base = (cand_index * n_hist + hist_index) * blocks
    length_mine = jnp.where(first_core, lengths[0], lengths[1])
    count_mine = jnp.where(first_core, counts[0], counts[1])
    key_tile = min(1024, blocks)
    key_tiles = blocks // key_tile
    request = jnp.stack([hist_index, 1 - hist_index]).astype(jnp.int32)
    counts_r = jnp.take(counts, request)
    keys_live = jnp.clip(jnp.take(lengths, request) - key_base, 0, blocks)
    last_tile = jnp.clip((keys_live + key_tile - 1) // key_tile - 1, 0, key_tiles - 1)
    row_base = ((cand_index - jnp.arange(n_cand)) % n_cand) * row_count
    rows_live = jnp.clip(counts_r[None, :] - row_base[:, None], 0, row_count)
    table = jnp.stack(
        [
            rows_live,
            jnp.broadcast_to(keys_live, rows_live.shape),
            jnp.broadcast_to(request, rows_live.shape),
            jnp.broadcast_to(last_tile, rows_live.shape),
        ],
        axis=-1,
    ).astype(jnp.int32).reshape(-1)

    own_partner = lax.ppermute(query_mine, "hist", swap(n_hist))
    own_sum = None
    acc = None
    forward = query_mine
    previous = None
    for k in list(range(1, n_cand)) + [0]:
        if k > 0:
            query_k = lax.ppermute(forward, "cand", ring(n_cand))
            if previous is not None:
                query_k, _ = lax.optimization_barrier((query_k, previous))
            forward = query_k
            query_partner = lax.ppermute(query_k, "hist", swap(n_hist))
        else:
            query_k, query_partner = query_mine, own_partner
        part_mine, part_other = attend(
            query_k, query_partner, hist_keys, hist_values, table, 8 * k, head_dim
        )
        previous = part_mine
        chip_sum = part_mine + lax.ppermute(part_other, "hist", swap(n_hist))
        if k == 0:
            own_sum = chip_sum
        else:
            if acc is not None:
                chip_sum = chip_sum + acc.astype(jnp.float32)
            acc = lax.ppermute(chip_sum.astype(jnp.bfloat16), "cand", ring(n_cand))
    total = own_sum if acc is None else own_sum + acc.astype(jnp.float32)

    attended = total / length_mine.astype(jnp.float32)
    moments = ring_sum(
        jnp.stack([jnp.sum(attended, axis=-1), jnp.sum(attended * attended, axis=-1)]),
        "head",
        n_head,
    )
    row_mean = moments[0][:, None] / width
    row_square = moments[1][:, None] / width
    normed_out = (attended - row_mean) * lax.rsqrt(row_square - row_mean * row_mean + 1e-05)
    gated = (normed_out * gate_u.astype(jnp.float32)).astype(jnp.bfloat16)
    partial_out = jnp.dot(gated, w_out, preferred_element_type=jnp.float32)
    slice_width = width // n_head
    chunks = partial_out.reshape(row_count, n_head, slice_width).transpose(1, 0, 2)
    summed = ring_reduce_scatter(chunks, "head", n_head, head_index)
    residual = lax.dynamic_slice_in_dim(cand_wide, head_index * slice_width, slice_width, 1)
    row_ids = cand_index * row_count + jnp.arange(row_count, dtype=jnp.int32)
    result = jnp.where((row_ids < count_mine)[:, None], residual + summed, 0.0).astype(jnp.bfloat16)
    result_other = lax.ppermute(result, "hist", swap(n_hist))
    first = jnp.where(first_core, result, result_other)
    second = jnp.where(first_core, result_other, result)
    return jnp.stack([first, second])


def solution(mesh):
    in_specs = (
        P("grp", "cand", None),
        P(None, None, "head"),
        P("head", None),
        P("grp", ("cand", "hist"), "head"),
        P("grp", ("cand", "hist"), "head"),
        P("grp"),
        P("grp"),
    )
    out_specs = P("grp", "cand", "head")
    return jax.shard_map(shards, mesh=mesh, in_specs=in_specs, out_specs=out_specs, check_vma=False)
```

```python
import functools
import math

import jax
import jax.numpy as jnp
from jax import lax
from jax.experimental import pallas as pl
from jax.experimental.pallas import tpu as pltpu
from jax.sharding import PartitionSpec as P

HEADS = 16
LANES = 128


def layer_norm_rows(values, width):
    row_mean = jnp.sum(values, axis=-1, keepdims=True) / width
    row_square = jnp.sum(values * values, axis=-1, keepdims=True) / width
    return (values - row_mean) * lax.rsqrt(row_square - row_mean * row_mean + 1e-05)


def ring(n):
    return [(i, (i + 1) % n) for i in range(n)]


def swap(n):
    return [(i, n - 1 - i) for i in range(n)]


def attend_kernel(limits, *refs, count, offset, head_dim, row_tile, key_tile):
    q_refs = refs[:count]
    k_ref, v_ref = refs[count:count + 2]
    o_refs = refs[count + 2:]
    r = pl.program_id(0)
    kv = pl.program_id(1)
    row_count, width = q_refs[0].shape
    half_scale = 0.5 / math.sqrt(head_dim)

    def compute(q_ref, o_ref, rows, keys_live):
        lane = lax.broadcasted_iota(jnp.int32, (1, LANES), 1)
        column = kv * key_tile + lax.broadcasted_iota(jnp.int32, (1, key_tile), 1)
        valid = column < keys_live

        def pair(p, carry):
            lanes = pl.ds(pl.multiple_of(p * LANES, LANES), LANES)
            q_pair = q_ref[0:rows, lanes]
            k_pair = k_ref[:, lanes]
            v_pair = v_ref[:, lanes]
            heads = LANES // head_dim
            head_of_lane = lane // head_dim
            q_stack = jnp.concatenate(
                [jnp.where(head_of_lane == hh, q_pair, jnp.zeros_like(q_pair)) for hh in range(heads)],
                axis=0,
            )
            scores = lax.dot_general(
                q_stack, k_pair, (((1,), (1,)), ((), ())), preferred_element_type=jnp.float32
            )
            halves = scores * half_scale
            weights = jnp.where(valid, halves + halves * jnp.tanh(halves), 0.0).astype(jnp.bfloat16)
            mixed = jnp.dot(weights, v_pair, preferred_element_type=jnp.float32)
            out = mixed[0:rows]
            for hh in range(1, heads):
                out = jnp.where(head_of_lane == hh, mixed[hh * rows:(hh + 1) * rows], out)
            o_ref[0:rows, lanes] += out
            return carry

        lax.fori_loop(0, width // LANES, pair, 0)

    def request(which, q_ref, o_ref):
        rows_live = limits[offset + 4 * which]
        keys_live = limits[offset + 4 * which + 1]

        @pl.when((r == 0) & (kv == 0))
        def _():
            o_ref[...] = jnp.zeros((row_count, width), jnp.float32)

        live = (r == which) & (kv * key_tile < keys_live)
        if row_count > row_tile:
            pl.when(live & (rows_live > row_tile))(
                lambda: compute(q_ref, o_ref, row_count, keys_live)
            )
            pl.when(live & (rows_live > 0) & (rows_live <= row_tile))(
                lambda: compute(q_ref, o_ref, row_tile, keys_live)
            )
        else:
            pl.when(live & (rows_live > 0))(lambda: compute(q_ref, o_ref, row_count, keys_live))

    for which in range(count):
        request(which, q_refs[which], o_refs[which])


def attend(queries, hist_keys, hist_values, table, offset, head_dim):
    count = len(queries)
    row_count, width = queries[0].shape
    key_count = hist_values.shape[1]
    row_tile = min(128, row_count)
    key_tile = min(1024, key_count)
    key_tiles = key_count // key_tile
    kernel = functools.partial(
        attend_kernel, count=count, offset=offset, head_dim=head_dim, row_tile=row_tile,
        key_tile=key_tile,
    )

    def kv_index(r, kv, lim):
        return (lim[offset + 4 * r + 2], jnp.minimum(kv, lim[offset + 4 * r + 3]), 0)

    flops = 4 * count * row_count * key_count * width
    out = jax.ShapeDtypeStruct((row_count, width), jnp.float32)
    whole = pl.BlockSpec((row_count, width), lambda r, kv, lim: (0, 0))
    return pl.pallas_call(
        kernel,
        out_shape=(out,) * count,
        grid_spec=pltpu.PrefetchScalarGridSpec(
            num_scalar_prefetch=1,
            grid=(count, key_tiles),
            in_specs=[whole] * count + [
                pl.BlockSpec((None, key_tile, width), kv_index),
                pl.BlockSpec((None, key_tile, width), kv_index),
            ],
            out_specs=(whole,) * count,
        ),
        cost_estimate=pl.CostEstimate(
            flops=flops,
            transcendentals=count * row_count * key_count * (width // head_dim),
            bytes_accessed=2 * count * key_count * width * 2 + count * row_count * width * 6,
        ),
    )(table, *queries, hist_keys, hist_values)


def ring_reduce_scatter(chunks, axis, n, index):
    acc = None
    for t in range(1, n):
        part = lax.dynamic_index_in_dim(chunks, (index - t) % n, 0, keepdims=False)
        if acc is not None:
            part = part + acc.astype(jnp.float32)
        acc = lax.ppermute(part.astype(jnp.bfloat16), axis, ring(n))
    own = lax.dynamic_index_in_dim(chunks, index, 0, keepdims=False)
    return own if acc is None else own + acc.astype(jnp.float32)


def ring_sum(values, axis, n):
    total = values
    moving = values
    for _ in range(1, n):
        moving = lax.ppermute(moving, axis, ring(n))
        total = total + moving
    return total


def shards(candidates, w_in, w_out, hist_keys, hist_values, lengths, counts):
    requests, row_count, width = candidates.shape
    width_here = w_in.shape[2]
    head_dim = width // HEADS
    n_cand = lax.axis_size("cand")
    n_hist = lax.axis_size("hist")
    n_head = lax.axis_size("head")
    cand_index = lax.axis_index("cand")
    hist_index = lax.axis_index("hist")
    head_index = lax.axis_index("head")
    assert n_hist == 2 and requests == 2
    first_core = hist_index == 0

    cand_mine = jnp.where(first_core, candidates[0], candidates[1])
    cand_wide = cand_mine.astype(jnp.float32)
    normed = layer_norm_rows(cand_wide, width).astype(jnp.bfloat16)
    projected = jnp.dot(
        normed, w_in.reshape(width, 2 * width_here), preferred_element_type=jnp.float32
    )
    activated = jax.nn.silu(projected).astype(jnp.bfloat16).reshape(row_count, 2, width_here)
    gate_u = activated[:, 0, :]
    query_mine = activated[:, 1, :]

    blocks = hist_keys.shape[1]
    key_base = (cand_index * n_hist + hist_index) * blocks
    length_mine = jnp.where(first_core, lengths[0], lengths[1])
    count_mine = jnp.where(first_core, counts[0], counts[1])
    key_tile = min(1024, blocks)
    key_tiles = blocks // key_tile
    request = jnp.stack([hist_index, 1 - hist_index]).astype(jnp.int32)
    counts_r = jnp.take(counts, request)
    keys_live = jnp.clip(jnp.take(lengths, request) - key_base, 0, blocks)
    last_tile = jnp.clip((keys_live + key_tile - 1) // key_tile - 1, 0, key_tiles - 1)
    row_base = ((cand_index - jnp.arange(n_cand)) % n_cand) * row_count
    rows_live = jnp.clip(counts_r[None, :] - row_base[:, None], 0, row_count)
    table = jnp.stack(
        [
            rows_live,
            jnp.broadcast_to(keys_live, rows_live.shape),
            jnp.broadcast_to(request, rows_live.shape),
            jnp.broadcast_to(last_tile, rows_live.shape),
        ],
        axis=-1,
    ).astype(jnp.int32).reshape(-1)

    own_partner = lax.ppermute(query_mine, "hist", swap(n_hist))
    (own_mine,) = attend((query_mine,), hist_keys, hist_values, table, 0, head_dim)
    acc = None
    forward = query_mine
    previous = own_mine
    for k in range(1, n_cand):
        query_k = lax.ppermute(forward, "cand", ring(n_cand))
        query_k, _ = lax.optimization_barrier((query_k, previous))
        forward = query_k
        query_partner = lax.ppermute(query_k, "hist", swap(n_hist))
        part_mine, part_other = attend(
            (query_k, query_partner), hist_keys, hist_values, table, 8 * k, head_dim
        )
        previous = part_mine
        chip_sum = part_mine + lax.ppermute(part_other, "hist", swap(n_hist))
        if acc is not None:
            chip_sum = chip_sum + acc.astype(jnp.float32)
        acc = lax.ppermute(chip_sum.astype(jnp.bfloat16), "cand", ring(n_cand))
    (own_other,) = attend((own_partner,), hist_keys, hist_values, table, 4, head_dim)
    own_sum = own_mine + lax.ppermute(own_other, "hist", swap(n_hist))
    total = own_sum if acc is None else own_sum + acc.astype(jnp.float32)

    attended = total / length_mine.astype(jnp.float32)
    moments = ring_sum(
        jnp.stack([jnp.sum(attended, axis=-1), jnp.sum(attended * attended, axis=-1)]),
        "head",
        n_head,
    )
    row_mean = moments[0][:, None] / width
    row_square = moments[1][:, None] / width
    normed_out = (attended - row_mean) * lax.rsqrt(row_square - row_mean * row_mean + 1e-05)
    gated = (normed_out * gate_u.astype(jnp.float32)).astype(jnp.bfloat16)
    partial_out = jnp.dot(gated, w_out, preferred_element_type=jnp.float32)
    slice_width = width // n_head
    chunks = partial_out.reshape(row_count, n_head, slice_width).transpose(1, 0, 2)
    summed = ring_reduce_scatter(chunks, "head", n_head, head_index)
    residual = lax.dynamic_slice_in_dim(cand_wide, head_index * slice_width, slice_width, 1)
    row_ids = cand_index * row_count + jnp.arange(row_count, dtype=jnp.int32)
    result = jnp.where((row_ids < count_mine)[:, None], residual + summed, 0.0).astype(jnp.bfloat16)
    result_other = lax.ppermute(result, "hist", swap(n_hist))
    first = jnp.where(first_core, result, result_other)
    second = jnp.where(first_core, result_other, result)
    return jnp.stack([first, second])


def solution(mesh):
    in_specs = (
        P("grp", "cand", None),
        P(None, None, "head"),
        P("head", None),
        P("grp", ("cand", "hist"), "head"),
        P("grp", ("cand", "hist"), "head"),
        P("grp"),
        P("grp"),
    )
    out_specs = P("grp", "cand", "head")
    return jax.shard_map(shards, mesh=mesh, in_specs=in_specs, out_specs=out_specs, check_vma=False)
```

```python
import functools
import math

import jax
import jax.numpy as jnp
from jax import lax
from jax.experimental import pallas as pl
from jax.experimental.pallas import tpu as pltpu
from jax.sharding import PartitionSpec as P

HEADS = 16
LANES = 128


def layer_norm_rows(values, width):
    row_mean = jnp.sum(values, axis=-1, keepdims=True) / width
    row_square = jnp.sum(values * values, axis=-1, keepdims=True) / width
    return (values - row_mean) * lax.rsqrt(row_square - row_mean * row_mean + 1e-05)


def ring(n):
    return [(i, (i + 1) % n) for i in range(n)]


def swap(n):
    return [(i, n - 1 - i) for i in range(n)]


def attend_kernel(limits, *refs, count, offset, head_dim, row_tile, key_tile):
    q_refs = refs[:count]
    k_ref, v_ref = refs[count:count + 2]
    o_refs = refs[count + 2:]
    r = pl.program_id(0)
    kv = pl.program_id(1)
    row_count, width = q_refs[0].shape
    half_scale = 0.5 / math.sqrt(head_dim)

    def compute(q_ref, o_ref, rows, keys_live):
        lane = lax.broadcasted_iota(jnp.int32, (1, LANES), 1)
        column = kv * key_tile + lax.broadcasted_iota(jnp.int32, (1, key_tile), 1)
        valid = column < keys_live

        def pair(p, carry):
            lanes = pl.ds(pl.multiple_of(p * LANES, LANES), LANES)
            q_pair = q_ref[0:rows, lanes]
            k_pair = k_ref[:, lanes]
            v_pair = v_ref[:, lanes]
            heads = LANES // head_dim
            head_of_lane = lane // head_dim
            q_stack = jnp.concatenate(
                [jnp.where(head_of_lane == hh, q_pair, jnp.zeros_like(q_pair)) for hh in range(heads)],
                axis=0,
            )
            scores = lax.dot_general(
                q_stack, k_pair, (((1,), (1,)), ((), ())), preferred_element_type=jnp.float32
            )
            halves = scores * half_scale
            weights = jnp.where(valid, halves + halves * jnp.tanh(halves), 0.0).astype(jnp.bfloat16)
            mixed = jnp.dot(weights, v_pair, preferred_element_type=jnp.float32)
            out = mixed[0:rows]
            for hh in range(1, heads):
                out = jnp.where(head_of_lane == hh, mixed[hh * rows:(hh + 1) * rows], out)
            o_ref[0:rows, lanes] += out
            return carry

        lax.fori_loop(0, width // LANES, pair, 0)

    def request(which, q_ref, o_ref):
        rows_live = limits[offset + 4 * which]
        keys_live = limits[offset + 4 * which + 1]

        @pl.when((r == 0) & (kv == 0))
        def _():
            o_ref[...] = jnp.zeros((row_count, width), jnp.float32)

        live = (r == which) & (kv * key_tile < keys_live)
        if row_count > row_tile:
            pl.when(live & (rows_live > row_tile))(
                lambda: compute(q_ref, o_ref, row_count, keys_live)
            )
            pl.when(live & (rows_live > 0) & (rows_live <= row_tile))(
                lambda: compute(q_ref, o_ref, row_tile, keys_live)
            )
        else:
            pl.when(live & (rows_live > 0))(lambda: compute(q_ref, o_ref, row_count, keys_live))

    for which in range(count):
        request(which, q_refs[which], o_refs[which])


def attend(queries, hist_keys, hist_values, table, offset, head_dim):
    count = len(queries)
    row_count, width = queries[0].shape
    key_count = hist_values.shape[1]
    row_tile = min(128, row_count)
    key_tile = min(1024, key_count)
    key_tiles = key_count // key_tile
    kernel = functools.partial(
        attend_kernel, count=count, offset=offset, head_dim=head_dim, row_tile=row_tile,
        key_tile=key_tile,
    )

    def kv_index(r, kv, lim):
        return (lim[offset + 4 * r + 2], jnp.minimum(kv, lim[offset + 4 * r + 3]), 0)

    flops = 4 * count * row_count * key_count * width
    out = jax.ShapeDtypeStruct((row_count, width), jnp.float32)
    whole = pl.BlockSpec((row_count, width), lambda r, kv, lim: (0, 0))
    return pl.pallas_call(
        kernel,
        out_shape=(out,) * count,
        grid_spec=pltpu.PrefetchScalarGridSpec(
            num_scalar_prefetch=1,
            grid=(count, key_tiles),
            in_specs=[whole] * count + [
                pl.BlockSpec((None, key_tile, width), kv_index),
                pl.BlockSpec((None, key_tile, width), kv_index),
            ],
            out_specs=(whole,) * count,
        ),
        cost_estimate=pl.CostEstimate(
            flops=flops,
            transcendentals=count * row_count * key_count * (width // head_dim),
            bytes_accessed=2 * count * key_count * width * 2 + count * row_count * width * 6,
        ),
    )(table, *queries, hist_keys, hist_values)


def ring_reduce_scatter(chunks, axis, n, index):
    acc = None
    for t in range(1, n):
        part = lax.dynamic_index_in_dim(chunks, (index - t) % n, 0, keepdims=False)
        if acc is not None:
            part = part + acc.astype(jnp.float32)
        acc = lax.ppermute(part.astype(jnp.bfloat16), axis, ring(n))
    own = lax.dynamic_index_in_dim(chunks, index, 0, keepdims=False)
    return own if acc is None else own + acc.astype(jnp.float32)


def ring_sum(values, axis, n):
    total = values
    moving = values
    for _ in range(1, n):
        moving = lax.ppermute(moving, axis, ring(n))
        total = total + moving
    return total


def shards(candidates, w_in, w_out, hist_keys, hist_values, lengths, counts):
    requests, row_count, width = candidates.shape
    width_here = w_in.shape[2]
    head_dim = width // HEADS
    n_cand = lax.axis_size("cand")
    n_hist = lax.axis_size("hist")
    n_head = lax.axis_size("head")
    cand_index = lax.axis_index("cand")
    hist_index = lax.axis_index("hist")
    head_index = lax.axis_index("head")
    assert n_hist == 2 and requests == 2
    first_core = hist_index == 0

    cand_mine = jnp.where(first_core, candidates[0], candidates[1])
    cand_wide = cand_mine.astype(jnp.float32)
    normed = layer_norm_rows(cand_wide, width).astype(jnp.bfloat16)
    projected = jnp.dot(
        normed, w_in.reshape(width, 2 * width_here), preferred_element_type=jnp.float32
    )
    activated = jax.nn.silu(projected).astype(jnp.bfloat16).reshape(row_count, 2, width_here)
    gate_u = activated[:, 0, :]
    query_mine = activated[:, 1, :]

    blocks = hist_keys.shape[1]
    key_base = (cand_index * n_hist + hist_index) * blocks
    length_mine = jnp.where(first_core, lengths[0], lengths[1])
    count_mine = jnp.where(first_core, counts[0], counts[1])
    key_tile = min(1024, blocks)
    key_tiles = blocks // key_tile
    request = jnp.stack([hist_index, 1 - hist_index]).astype(jnp.int32)
    counts_r = jnp.take(counts, request)
    keys_live = jnp.clip(jnp.take(lengths, request) - key_base, 0, blocks)
    last_tile = jnp.clip((keys_live + key_tile - 1) // key_tile - 1, 0, key_tiles - 1)
    row_base = ((cand_index - jnp.arange(n_cand)) % n_cand) * row_count
    rows_live = jnp.clip(counts_r[None, :] - row_base[:, None], 0, row_count)
    table = jnp.stack(
        [
            rows_live,
            jnp.broadcast_to(keys_live, rows_live.shape),
            jnp.broadcast_to(request, rows_live.shape),
            jnp.broadcast_to(last_tile, rows_live.shape),
        ],
        axis=-1,
    ).astype(jnp.int32).reshape(-1)

    own_partner = lax.ppermute(query_mine, "hist", swap(n_hist))
    (own_mine,) = attend((query_mine,), hist_keys, hist_values, table, 0, head_dim)
    acc = None
    sent = None
    forward = query_mine
    previous = own_mine
    for k in range(1, n_cand):
        query_k = lax.ppermute(forward, "cand", ring(n_cand))
        query_k, _ = lax.optimization_barrier((query_k, previous if sent is None else sent))
        forward = query_k
        query_partner = lax.ppermute(query_k, "hist", swap(n_hist))
        part_mine, part_other = attend(
            (query_k, query_partner), hist_keys, hist_values, table, 8 * k, head_dim
        )
        previous = part_mine
        chip_sum = part_mine + lax.ppermute(part_other, "hist", swap(n_hist))
        if acc is not None:
            chip_sum = chip_sum + acc.astype(jnp.float32)
        sent = chip_sum.astype(jnp.bfloat16)
        acc = lax.ppermute(sent, "cand", ring(n_cand))
    (own_other,) = attend((own_partner,), hist_keys, hist_values, table, 4, head_dim)
    own_sum = own_mine + lax.ppermute(own_other, "hist", swap(n_hist))
    total = own_sum if acc is None else own_sum + acc.astype(jnp.float32)

    attended = total / length_mine.astype(jnp.float32)
    moments = ring_sum(
        jnp.stack([jnp.sum(attended, axis=-1), jnp.sum(attended * attended, axis=-1)]),
        "head",
        n_head,
    )
    row_mean = moments[0][:, None] / width
    row_square = moments[1][:, None] / width
    normed_out = (attended - row_mean) * lax.rsqrt(row_square - row_mean * row_mean + 1e-05)
    gated = (normed_out * gate_u.astype(jnp.float32)).astype(jnp.bfloat16)
    partial_out = jnp.dot(gated, w_out, preferred_element_type=jnp.float32)
    slice_width = width // n_head
    chunks = partial_out.reshape(row_count, n_head, slice_width).transpose(1, 0, 2)
    summed = ring_reduce_scatter(chunks, "head", n_head, head_index)
    residual = lax.dynamic_slice_in_dim(cand_wide, head_index * slice_width, slice_width, 1)
    row_ids = cand_index * row_count + jnp.arange(row_count, dtype=jnp.int32)
    result = jnp.where((row_ids < count_mine)[:, None], residual + summed, 0.0).astype(jnp.bfloat16)
    result_other = lax.ppermute(result, "hist", swap(n_hist))
    first = jnp.where(first_core, result, result_other)
    second = jnp.where(first_core, result_other, result)
    return jnp.stack([first, second])


def solution(mesh):
    in_specs = (
        P("grp", "cand", None),
        P(None, None, "head"),
        P("head", None),
        P("grp", ("cand", "hist"), "head"),
        P("grp", ("cand", "hist"), "head"),
        P("grp"),
        P("grp"),
    )
    out_specs = P("grp", "cand", "head")
    return jax.shard_map(shards, mesh=mesh, in_specs=in_specs, out_specs=out_specs, check_vma=False)
```

```python
import functools
import math

import jax
import jax.numpy as jnp
from jax import lax
from jax.experimental import pallas as pl
from jax.experimental.pallas import tpu as pltpu
from jax.sharding import PartitionSpec as P

HEADS = 16
LANES = 128


def layer_norm_rows(values, width):
    row_mean = jnp.sum(values, axis=-1, keepdims=True) / width
    row_square = jnp.sum(values * values, axis=-1, keepdims=True) / width
    return (values - row_mean) * lax.rsqrt(row_square - row_mean * row_mean + 1e-05)


def ring(n):
    return [(i, (i + 1) % n) for i in range(n)]


def swap(n):
    return [(i, n - 1 - i) for i in range(n)]


def attend_kernel(limits, *refs, count, offset, head_dim, row_tile, key_tile):
    q_refs = refs[:count]
    k_ref, v_ref = refs[count:count + 2]
    o_refs = refs[count + 2:]
    r = pl.program_id(0)
    kv = pl.program_id(1)
    row_count, width = q_refs[0].shape
    half_scale = 0.5 / math.sqrt(head_dim)

    def compute(q_ref, o_ref, rows, keys_live):
        lane = lax.broadcasted_iota(jnp.int32, (1, LANES), 1)
        column = kv * key_tile + lax.broadcasted_iota(jnp.int32, (1, key_tile), 1)
        valid = column < keys_live

        def pair(p, carry):
            lanes = pl.ds(pl.multiple_of(p * LANES, LANES), LANES)
            q_pair = q_ref[0:rows, lanes]
            k_pair = k_ref[:, lanes]
            v_pair = v_ref[:, lanes]
            heads = LANES // head_dim
            head_of_lane = lane // head_dim
            q_stack = jnp.concatenate(
                [jnp.where(head_of_lane == hh, q_pair, jnp.zeros_like(q_pair)) for hh in range(heads)],
                axis=0,
            )
            scores = lax.dot_general(
                q_stack, k_pair, (((1,), (1,)), ((), ())), preferred_element_type=jnp.float32
            )
            halves = scores * half_scale
            weights = jnp.where(valid, halves + halves * jnp.tanh(halves), 0.0).astype(jnp.bfloat16)
            mixed = jnp.dot(weights, v_pair, preferred_element_type=jnp.float32)
            out = mixed[0:rows]
            for hh in range(1, heads):
                out = jnp.where(head_of_lane == hh, mixed[hh * rows:(hh + 1) * rows], out)
            o_ref[0:rows, lanes] += out
            return carry

        lax.fori_loop(0, width // LANES, pair, 0)

    def request(which, q_ref, o_ref):
        rows_live = limits[offset + 4 * which]
        keys_live = limits[offset + 4 * which + 1]

        @pl.when((r == 0) & (kv == 0))
        def _():
            o_ref[...] = jnp.zeros((row_count, width), jnp.float32)

        live = (r == which) & (kv * key_tile < keys_live)
        if row_count > row_tile:
            pl.when(live & (rows_live > row_tile))(
                lambda: compute(q_ref, o_ref, row_count, keys_live)
            )
            pl.when(live & (rows_live > 0) & (rows_live <= row_tile))(
                lambda: compute(q_ref, o_ref, row_tile, keys_live)
            )
        else:
            pl.when(live & (rows_live > 0))(lambda: compute(q_ref, o_ref, row_count, keys_live))

    for which in range(count):
        request(which, q_refs[which], o_refs[which])


def attend(queries, hist_keys, hist_values, table, offset, head_dim):
    count = len(queries)
    row_count, width = queries[0].shape
    key_count = hist_values.shape[1]
    row_tile = min(128, row_count)
    key_tile = min(1024, key_count)
    key_tiles = key_count // key_tile
    kernel = functools.partial(
        attend_kernel, count=count, offset=offset, head_dim=head_dim, row_tile=row_tile,
        key_tile=key_tile,
    )

    def kv_index(r, kv, lim):
        return (lim[offset + 4 * r + 2], jnp.minimum(kv, lim[offset + 4 * r + 3]), 0)

    flops = 4 * count * row_count * key_count * width
    out = jax.ShapeDtypeStruct((row_count, width), jnp.float32)
    whole = pl.BlockSpec((row_count, width), lambda r, kv, lim: (0, 0))
    return pl.pallas_call(
        kernel,
        out_shape=(out,) * count,
        grid_spec=pltpu.PrefetchScalarGridSpec(
            num_scalar_prefetch=1,
            grid=(count, key_tiles),
            in_specs=[whole] * count + [
                pl.BlockSpec((None, key_tile, width), kv_index),
                pl.BlockSpec((None, key_tile, width), kv_index),
            ],
            out_specs=(whole,) * count,
        ),
        cost_estimate=pl.CostEstimate(
            flops=flops,
            transcendentals=count * row_count * key_count * (width // head_dim),
            bytes_accessed=2 * count * key_count * width * 2 + count * row_count * width * 6,
        ),
    )(table, *queries, hist_keys, hist_values)


def ring_reduce_scatter(chunks, axis, n, index):
    acc = None
    for t in range(1, n):
        part = lax.dynamic_index_in_dim(chunks, (index - t) % n, 0, keepdims=False)
        if acc is not None:
            part = part + acc.astype(jnp.float32)
        acc = lax.ppermute(part.astype(jnp.bfloat16), axis, ring(n))
    own = lax.dynamic_index_in_dim(chunks, index, 0, keepdims=False)
    return own if acc is None else own + acc.astype(jnp.float32)


def ring_sum(values, axis, n):
    total = values
    moving = values
    for _ in range(1, n):
        moving = lax.ppermute(moving, axis, ring(n))
        total = total + moving
    return total


def shards(candidates, w_in, w_out, hist_keys, hist_values, lengths, counts):
    requests, row_count, width = candidates.shape
    width_here = w_in.shape[2]
    head_dim = width // HEADS
    n_cand = lax.axis_size("cand")
    n_hist = lax.axis_size("hist")
    n_head = lax.axis_size("head")
    cand_index = lax.axis_index("cand")
    hist_index = lax.axis_index("hist")
    head_index = lax.axis_index("head")
    assert n_hist == 2 and requests == 2
    first_core = hist_index == 0

    cand_mine = jnp.where(first_core, candidates[0], candidates[1])
    cand_wide = cand_mine.astype(jnp.float32)
    normed = layer_norm_rows(cand_wide, width).astype(jnp.bfloat16)
    projected = jnp.einsum("cd,dgf->gcf", normed, w_in, preferred_element_type=jnp.float32)
    activated = jax.nn.silu(projected).astype(jnp.bfloat16)
    gate_u = activated[0]
    query_mine = activated[1]

    blocks = hist_keys.shape[1]
    key_base = (cand_index * n_hist + hist_index) * blocks
    length_mine = jnp.where(first_core, lengths[0], lengths[1])
    count_mine = jnp.where(first_core, counts[0], counts[1])
    key_tile = min(1024, blocks)
    key_tiles = blocks // key_tile
    request = jnp.stack([hist_index, 1 - hist_index]).astype(jnp.int32)
    counts_r = jnp.where(first_core, counts, counts[::-1])
    keys_live = jnp.clip(jnp.where(first_core, lengths, lengths[::-1]) - key_base, 0, blocks)
    last_tile = jnp.clip((keys_live + key_tile - 1) // key_tile - 1, 0, key_tiles - 1)
    row_base = ((cand_index - jnp.arange(n_cand)) % n_cand) * row_count
    rows_live = jnp.clip(counts_r[None, :] - row_base[:, None], 0, row_count)
    table = jnp.stack(
        [
            rows_live,
            jnp.broadcast_to(keys_live, rows_live.shape),
            jnp.broadcast_to(request, rows_live.shape),
            jnp.broadcast_to(last_tile, rows_live.shape),
        ],
        axis=-1,
    ).astype(jnp.int32).reshape(-1)

    own_partner = lax.ppermute(query_mine, "hist", swap(n_hist))
    (own_mine,) = attend((query_mine,), hist_keys, hist_values, table, 0, head_dim)
    acc = None
    forward = query_mine
    previous = own_mine
    for k in range(1, n_cand):
        query_k = lax.ppermute(forward, "cand", ring(n_cand))
        query_k, _ = lax.optimization_barrier((query_k, previous))
        forward = query_k
        query_partner = lax.ppermute(query_k, "hist", swap(n_hist))
        part_mine, part_other = attend(
            (query_k, query_partner), hist_keys, hist_values, table, 8 * k, head_dim
        )
        previous = part_mine
        chip_sum = part_mine + lax.ppermute(part_other, "hist", swap(n_hist))
        if acc is not None:
            chip_sum = chip_sum + acc.astype(jnp.float32)
        acc = lax.ppermute(chip_sum.astype(jnp.bfloat16), "cand", ring(n_cand))
    (own_other,) = attend((own_partner,), hist_keys, hist_values, table, 4, head_dim)
    own_sum = own_mine + lax.ppermute(own_other, "hist", swap(n_hist))
    total = own_sum if acc is None else own_sum + acc.astype(jnp.float32)

    attended = total / length_mine.astype(jnp.float32)
    moments = ring_sum(
        jnp.stack([jnp.sum(attended, axis=-1), jnp.sum(attended * attended, axis=-1)]),
        "head",
        n_head,
    )
    row_mean = moments[0][:, None] / width
    row_square = moments[1][:, None] / width
    normed_out = (attended - row_mean) * lax.rsqrt(row_square - row_mean * row_mean + 1e-05)
    gated = (normed_out * gate_u.astype(jnp.float32)).astype(jnp.bfloat16)
    partial_out = jnp.dot(gated, w_out, preferred_element_type=jnp.float32)
    slice_width = width // n_head
    chunks = partial_out.reshape(row_count, n_head, slice_width).transpose(1, 0, 2)
    summed = ring_reduce_scatter(chunks, "head", n_head, head_index)
    residual = lax.dynamic_slice_in_dim(cand_wide, head_index * slice_width, slice_width, 1)
    row_ids = cand_index * row_count + jnp.arange(row_count, dtype=jnp.int32)
    result = jnp.where((row_ids < count_mine)[:, None], residual + summed, 0.0).astype(jnp.bfloat16)
    result_other = lax.ppermute(result, "hist", swap(n_hist))
    first = jnp.where(first_core, result, result_other)
    second = jnp.where(first_core, result_other, result)
    return jnp.stack([first, second])


def solution(mesh):
    in_specs = (
        P("grp", "cand", None),
        P(None, None, "head"),
        P("head", None),
        P("grp", ("cand", "hist"), "head"),
        P("grp", ("cand", "hist"), "head"),
        P("grp"),
        P("grp"),
    )
    out_specs = P("grp", "cand", "head")
    return jax.shard_map(shards, mesh=mesh, in_specs=in_specs, out_specs=out_specs, check_vma=False)
```

```python
import functools
import math

import jax
import jax.numpy as jnp
from jax import lax
from jax.experimental import pallas as pl
from jax.experimental.pallas import tpu as pltpu
from jax.sharding import PartitionSpec as P

HEADS = 16
LANES = 128


def layer_norm_rows(values, width):
    row_mean = jnp.sum(values, axis=-1, keepdims=True) / width
    row_square = jnp.sum(values * values, axis=-1, keepdims=True) / width
    return (values - row_mean) * lax.rsqrt(row_square - row_mean * row_mean + 1e-05)


def ring(n):
    return [(i, (i + 1) % n) for i in range(n)]


def swap(n):
    return [(i, n - 1 - i) for i in range(n)]


def attend_kernel(limits, *refs, count, offset, head_dim, row_tile, key_tile):
    q_refs = refs[:count]
    k_ref, v_ref = refs[count:count + 2]
    o_refs = refs[count + 2:]
    r = pl.program_id(0)
    kv = pl.program_id(1)
    row_count, width = q_refs[0].shape
    half_scale = 0.5 / math.sqrt(head_dim)

    def compute(q_ref, o_ref, rows, keys_live):
        lane = lax.broadcasted_iota(jnp.int32, (1, LANES), 1)
        column = kv * key_tile + lax.broadcasted_iota(jnp.int32, (1, key_tile), 1)
        valid = column < keys_live

        def pair(p, carry):
            lanes = pl.ds(pl.multiple_of(p * LANES, LANES), LANES)
            q_pair = q_ref[0:rows, lanes]
            k_pair = k_ref[:, lanes]
            v_pair = v_ref[:, lanes]
            heads = LANES // head_dim
            head_of_lane = lane // head_dim
            q_stack = jnp.concatenate(
                [jnp.where(head_of_lane == hh, q_pair, jnp.zeros_like(q_pair)) for hh in range(heads)],
                axis=0,
            )
            scores = lax.dot_general(
                q_stack, k_pair, (((1,), (1,)), ((), ())), preferred_element_type=jnp.float32
            )
            halves = scores * half_scale
            weights = jnp.where(valid, halves + halves * jnp.tanh(halves), 0.0).astype(jnp.bfloat16)
            mixed = jnp.dot(weights, v_pair, preferred_element_type=jnp.float32)
            out = mixed[0:rows]
            for hh in range(1, heads):
                out = jnp.where(head_of_lane == hh, mixed[hh * rows:(hh + 1) * rows], out)
            o_ref[0:rows, lanes] += out
            return carry

        lax.fori_loop(0, width // LANES, pair, 0)

    def request(which, q_ref, o_ref):
        rows_live = limits[offset + 4 * which]
        keys_live = limits[offset + 4 * which + 1]

        @pl.when((r == 0) & (kv == 0))
        def _():
            o_ref[...] = jnp.zeros((row_count, width), jnp.float32)

        live = (r == which) & (kv * key_tile < keys_live)
        if row_count > row_tile:
            pl.when(live & (rows_live > row_tile))(
                lambda: compute(q_ref, o_ref, row_count, keys_live)
            )
            pl.when(live & (rows_live > 0) & (rows_live <= row_tile))(
                lambda: compute(q_ref, o_ref, row_tile, keys_live)
            )
        else:
            pl.when(live & (rows_live > 0))(lambda: compute(q_ref, o_ref, row_count, keys_live))

    for which in range(count):
        request(which, q_refs[which], o_refs[which])


def attend(queries, hist_keys, hist_values, table, offset, head_dim):
    count = len(queries)
    row_count, width = queries[0].shape
    key_count = hist_values.shape[1]
    row_tile = min(128, row_count)
    key_tile = min(1024, key_count)
    key_tiles = key_count // key_tile
    kernel = functools.partial(
        attend_kernel, count=count, offset=offset, head_dim=head_dim, row_tile=row_tile,
        key_tile=key_tile,
    )

    def kv_index(r, kv, lim):
        return (lim[offset + 4 * r + 2], jnp.minimum(kv, lim[offset + 4 * r + 3]), 0)

    flops = 4 * count * row_count * key_count * width
    out = jax.ShapeDtypeStruct((row_count, width), jnp.float32)
    whole = pl.BlockSpec((row_count, width), lambda r, kv, lim: (0, 0))
    return pl.pallas_call(
        kernel,
        out_shape=(out,) * count,
        grid_spec=pltpu.PrefetchScalarGridSpec(
            num_scalar_prefetch=1,
            grid=(count, key_tiles),
            in_specs=[whole] * count + [
                pl.BlockSpec((None, key_tile, width), kv_index),
                pl.BlockSpec((None, key_tile, width), kv_index),
            ],
            out_specs=(whole,) * count,
        ),
        cost_estimate=pl.CostEstimate(
            flops=flops,
            transcendentals=count * row_count * key_count * (width // head_dim),
            bytes_accessed=2 * count * key_count * width * 2 + count * row_count * width * 6,
        ),
    )(table, *queries, hist_keys, hist_values)


def ring_reduce_scatter(chunks, axis, n, index):
    acc = None
    for t in range(1, n):
        part = lax.dynamic_index_in_dim(chunks, (index - t) % n, 0, keepdims=False)
        if acc is not None:
            part = part + acc.astype(jnp.float32)
        acc = lax.ppermute(part.astype(jnp.bfloat16), axis, ring(n))
    own = lax.dynamic_index_in_dim(chunks, index, 0, keepdims=False)
    return own if acc is None else own + acc.astype(jnp.float32)


def ring_sum(values, axis, n):
    total = values
    moving = values
    for _ in range(1, n):
        moving = lax.ppermute(moving, axis, ring(n))
        total = total + moving
    return total


def shards(candidates, w_in, w_out, hist_keys, hist_values, lengths, counts):
    requests, row_count, width = candidates.shape
    width_here = w_in.shape[2]
    head_dim = width // HEADS
    n_cand = lax.axis_size("cand")
    n_hist = lax.axis_size("hist")
    n_head = lax.axis_size("head")
    cand_index = lax.axis_index("cand")
    hist_index = lax.axis_index("hist")
    head_index = lax.axis_index("head")
    assert n_hist == 2 and requests == 2
    first_core = hist_index == 0

    cand_mine = jnp.where(first_core, candidates[0], candidates[1])
    cand_wide = cand_mine.astype(jnp.float32)
    normed = layer_norm_rows(cand_wide, width).astype(jnp.bfloat16)
    projected = jnp.dot(
        normed, w_in.reshape(width, 2 * width_here), preferred_element_type=jnp.float32
    )
    activated = jax.nn.silu(projected).astype(jnp.bfloat16).reshape(row_count, 2, width_here)
    gate_u = activated[:, 0, :]
    query_mine = activated[:, 1, :]

    blocks = hist_keys.shape[1]
    key_base = (cand_index * n_hist + hist_index) * blocks
    length_mine = jnp.where(first_core, lengths[0], lengths[1])
    count_mine = jnp.where(first_core, counts[0], counts[1])
    key_tile = min(1024, blocks)
    key_tiles = blocks // key_tile
    request = jnp.stack([hist_index, 1 - hist_index]).astype(jnp.int32)
    counts_r = jnp.take(counts, request)
    keys_live = jnp.clip(jnp.take(lengths, request) - key_base, 0, blocks)
    last_tile = jnp.clip((keys_live + key_tile - 1) // key_tile - 1, 0, key_tiles - 1)
    row_base = ((cand_index - jnp.arange(n_cand)) % n_cand) * row_count
    rows_live = jnp.clip(counts_r[None, :] - row_base[:, None], 0, row_count)
    table = jnp.stack(
        [
            rows_live,
            jnp.broadcast_to(keys_live, rows_live.shape),
            jnp.broadcast_to(request, rows_live.shape),
            jnp.broadcast_to(last_tile, rows_live.shape),
        ],
        axis=-1,
    ).astype(jnp.int32).reshape(-1)

    own_partner = lax.ppermute(query_mine, "hist", swap(n_hist))
    (own_mine,) = attend((query_mine,), hist_keys, hist_values, table, 0, head_dim)
    acc = None
    forward = query_mine
    previous = own_mine
    for k in range(1, n_cand):
        query_k = lax.ppermute(forward, "cand", ring(n_cand))
        query_k, _ = lax.optimization_barrier((query_k, previous))
        forward = query_k
        query_partner = lax.ppermute(query_k, "hist", swap(n_hist))
        part_mine, part_other = attend(
            (query_k, query_partner), hist_keys, hist_values, table, 8 * k, head_dim
        )
        previous = part_mine
        chip_sum = part_mine + lax.ppermute(part_other, "hist", swap(n_hist))
        if acc is not None:
            chip_sum = chip_sum + acc.astype(jnp.float32)
        acc = lax.ppermute(chip_sum.astype(jnp.bfloat16), "cand", ring(n_cand))
    (own_other,) = attend((own_partner,), hist_keys, hist_values, table, 4, head_dim)
    own_sum = own_mine + lax.ppermute(own_other, "hist", swap(n_hist))
    total = own_sum if acc is None else own_sum + acc.astype(jnp.float32)

    slice_width = width // n_head
    residual = lax.dynamic_slice_in_dim(cand_wide, head_index * slice_width, slice_width, 1)
    row_ids = cand_index * row_count + jnp.arange(row_count, dtype=jnp.int32)
    attended = total / length_mine.astype(jnp.float32)
    halves = 2 if row_count % 16 == 0 else 1
    part_rows = row_count // halves
    firsts, seconds = [], []
    for h in range(halves):
        rows = slice(h * part_rows, (h + 1) * part_rows)
        att = attended[rows]
        moments = ring_sum(
            jnp.stack([jnp.sum(att, axis=-1), jnp.sum(att * att, axis=-1)]), "head", n_head
        )
        row_mean = moments[0][:, None] / width
        row_square = moments[1][:, None] / width
        normed_out = (att - row_mean) * lax.rsqrt(row_square - row_mean * row_mean + 1e-05)
        gated = (normed_out * gate_u[rows].astype(jnp.float32)).astype(jnp.bfloat16)
        partial_out = jnp.dot(gated, w_out, preferred_element_type=jnp.float32)
        chunks = partial_out.reshape(part_rows, n_head, slice_width).transpose(1, 0, 2)
        summed = ring_reduce_scatter(chunks, "head", n_head, head_index)
        live = (row_ids[rows] < count_mine)[:, None]
        result = jnp.where(live, residual[rows] + summed, 0.0).astype(jnp.bfloat16)
        result_other = lax.ppermute(result, "hist", swap(n_hist))
        firsts.append(jnp.where(first_core, result, result_other))
        seconds.append(jnp.where(first_core, result_other, result))
    first = jnp.concatenate(firsts, axis=0)
    second = jnp.concatenate(seconds, axis=0)
    return jnp.stack([first, second])


def solution(mesh):
    in_specs = (
        P("grp", "cand", None),
        P(None, None, "head"),
        P("head", None),
        P("grp", ("cand", "hist"), "head"),
        P("grp", ("cand", "hist"), "head"),
        P("grp"),
        P("grp"),
    )
    out_specs = P("grp", "cand", "head")
    return jax.shard_map(shards, mesh=mesh, in_specs=in_specs, out_specs=out_specs, check_vma=False)
```

```python
import functools
import math

import jax
import jax.numpy as jnp
from jax import lax
from jax.experimental import pallas as pl
from jax.experimental.pallas import tpu as pltpu
from jax.sharding import PartitionSpec as P

HEADS = 16
LANES = 128


def layer_norm_rows(values, width):
    row_mean = jnp.sum(values, axis=-1, keepdims=True) / width
    row_square = jnp.sum(values * values, axis=-1, keepdims=True) / width
    return (values - row_mean) * lax.rsqrt(row_square - row_mean * row_mean + 1e-05)


def ring(n):
    return [(i, (i + 1) % n) for i in range(n)]


def swap(n):
    return [(i, n - 1 - i) for i in range(n)]


def attend_kernel(limits, *refs, count, offsets, head_dim, row_tile, key_tile):
    q_refs = refs[:count]
    k_ref, v_ref = refs[count:count + 2]
    o_refs = refs[count + 2:]
    r = pl.program_id(0)
    kv = pl.program_id(1)
    row_count, width = q_refs[0].shape
    half_scale = 0.5 / math.sqrt(head_dim)

    def compute(q_ref, o_ref, rows, keys_live):
        lane = lax.broadcasted_iota(jnp.int32, (1, LANES), 1)
        column = kv * key_tile + lax.broadcasted_iota(jnp.int32, (1, key_tile), 1)
        valid = column < keys_live

        def pair(p, carry):
            lanes = pl.ds(pl.multiple_of(p * LANES, LANES), LANES)
            q_pair = q_ref[0:rows, lanes]
            k_pair = k_ref[:, lanes]
            v_pair = v_ref[:, lanes]
            heads = LANES // head_dim
            head_of_lane = lane // head_dim
            q_stack = jnp.concatenate(
                [jnp.where(head_of_lane == hh, q_pair, jnp.zeros_like(q_pair)) for hh in range(heads)],
                axis=0,
            )
            scores = lax.dot_general(
                q_stack, k_pair, (((1,), (1,)), ((), ())), preferred_element_type=jnp.float32
            )
            halves = scores * half_scale
            weights = jnp.where(valid, halves + halves * jnp.tanh(halves), 0.0).astype(jnp.bfloat16)
            mixed = jnp.dot(weights, v_pair, preferred_element_type=jnp.float32)
            out = mixed[0:rows]
            for hh in range(1, heads):
                out = jnp.where(head_of_lane == hh, mixed[hh * rows:(hh + 1) * rows], out)
            o_ref[0:rows, lanes] += out
            return carry

        lax.fori_loop(0, width // LANES, pair, 0)

    def request(which, q_ref, o_ref):
        rows_live = limits[offsets[which]]
        keys_live = limits[offsets[which] + 1]

        @pl.when((r == 0) & (kv == 0))
        def _():
            o_ref[...] = jnp.zeros((row_count, width), jnp.float32)

        live = (r == which) & (kv * key_tile < keys_live)
        if row_count > row_tile:
            pl.when(live & (rows_live > row_tile))(
                lambda: compute(q_ref, o_ref, row_count, keys_live)
            )
            pl.when(live & (rows_live > 0) & (rows_live <= row_tile))(
                lambda: compute(q_ref, o_ref, row_tile, keys_live)
            )
        else:
            pl.when(live & (rows_live > 0))(lambda: compute(q_ref, o_ref, row_count, keys_live))

    for which in range(count):
        request(which, q_refs[which], o_refs[which])


def attend(queries, hist_keys, hist_values, table, offsets, head_dim):
    count = len(queries)
    row_count, width = queries[0].shape
    key_count = hist_values.shape[1]
    row_tile = min(128, row_count)
    key_tile = min(1024, key_count)
    key_tiles = key_count // key_tile
    kernel = functools.partial(
        attend_kernel, count=count, offsets=offsets, head_dim=head_dim, row_tile=row_tile,
        key_tile=key_tile,
    )

    def kv_index(r, kv, lim):
        base = offsets[-1]
        for i in range(count - 2, -1, -1):
            base = jnp.where(r == i, offsets[i], base)
        return (lim[base + 2], jnp.minimum(kv, lim[base + 3]), 0)

    flops = 4 * count * row_count * key_count * width
    out = jax.ShapeDtypeStruct((row_count, width), jnp.float32)
    whole = pl.BlockSpec((row_count, width), lambda r, kv, lim: (0, 0))
    return pl.pallas_call(
        kernel,
        out_shape=(out,) * count,
        grid_spec=pltpu.PrefetchScalarGridSpec(
            num_scalar_prefetch=1,
            grid=(count, key_tiles),
            in_specs=[whole] * count + [
                pl.BlockSpec((None, key_tile, width), kv_index),
                pl.BlockSpec((None, key_tile, width), kv_index),
            ],
            out_specs=(whole,) * count,
        ),
        cost_estimate=pl.CostEstimate(
            flops=flops,
            transcendentals=count * row_count * key_count * (width // head_dim),
            bytes_accessed=2 * count * key_count * width * 2 + count * row_count * width * 6,
        ),
    )(table, *queries, hist_keys, hist_values)


def ring_reduce_scatter(chunks, axis, n, index):
    acc = None
    for t in range(1, n):
        part = lax.dynamic_index_in_dim(chunks, (index - t) % n, 0, keepdims=False)
        if acc is not None:
            part = part + acc.astype(jnp.float32)
        acc = lax.ppermute(part.astype(jnp.bfloat16), axis, ring(n))
    own = lax.dynamic_index_in_dim(chunks, index, 0, keepdims=False)
    return own if acc is None else own + acc.astype(jnp.float32)


def ring_sum(values, axis, n):
    total = values
    moving = values
    for _ in range(1, n):
        moving = lax.ppermute(moving, axis, ring(n))
        total = total + moving
    return total


def shards(candidates, w_in, w_out, hist_keys, hist_values, lengths, counts):
    requests, row_count, width = candidates.shape
    width_here = w_in.shape[2]
    head_dim = width // HEADS
    n_cand = lax.axis_size("cand")
    n_hist = lax.axis_size("hist")
    n_head = lax.axis_size("head")
    cand_index = lax.axis_index("cand")
    hist_index = lax.axis_index("hist")
    head_index = lax.axis_index("head")
    assert n_hist == 2 and requests == 2
    first_core = hist_index == 0

    cand_mine = jnp.where(first_core, candidates[0], candidates[1])
    cand_wide = cand_mine.astype(jnp.float32)
    normed = layer_norm_rows(cand_wide, width).astype(jnp.bfloat16)
    projected = jnp.dot(
        normed, w_in.reshape(width, 2 * width_here), preferred_element_type=jnp.float32
    )
    activated = jax.nn.silu(projected).astype(jnp.bfloat16).reshape(row_count, 2, width_here)
    gate_u = activated[:, 0, :]
    query_mine = activated[:, 1, :]

    blocks = hist_keys.shape[1]
    key_base = (cand_index * n_hist + hist_index) * blocks
    length_mine = jnp.where(first_core, lengths[0], lengths[1])
    count_mine = jnp.where(first_core, counts[0], counts[1])
    key_tile = min(1024, blocks)
    key_tiles = blocks // key_tile
    request = jnp.stack([hist_index, 1 - hist_index]).astype(jnp.int32)
    counts_r = jnp.take(counts, request)
    keys_live = jnp.clip(jnp.take(lengths, request) - key_base, 0, blocks)
    last_tile = jnp.clip((keys_live + key_tile - 1) // key_tile - 1, 0, key_tiles - 1)
    row_base = ((cand_index - jnp.arange(n_cand)) % n_cand) * row_count
    rows_live = jnp.clip(counts_r[None, :] - row_base[:, None], 0, row_count)
    table = jnp.stack(
        [
            rows_live,
            jnp.broadcast_to(keys_live, rows_live.shape),
            jnp.broadcast_to(request, rows_live.shape),
            jnp.broadcast_to(last_tile, rows_live.shape),
        ],
        axis=-1,
    ).astype(jnp.int32).reshape(-1)

    own_partner = lax.ppermute(query_mine, "hist", swap(n_hist))
    (own_mine,) = attend((query_mine,), hist_keys, hist_values, table, (0,), head_dim)
    acc = None
    forward = query_mine
    previous = own_mine
    for k in range(1, n_cand):
        query_k = lax.ppermute(forward, "cand", ring(n_cand))
        query_k, _ = lax.optimization_barrier((query_k, previous))
        forward = query_k
        query_partner = lax.ppermute(query_k, "hist", swap(n_hist))
        if k < n_cand - 1:
            part_mine, part_other = attend(
                (query_k, query_partner), hist_keys, hist_values, table, (8 * k, 8 * k + 4), head_dim
            )
        else:
            part_mine, part_other, own_other = attend(
                (query_k, query_partner, own_partner), hist_keys, hist_values, table,
                (8 * k, 8 * k + 4, 4), head_dim,
            )
        previous = part_mine
        chip_sum = part_mine + lax.ppermute(part_other, "hist", swap(n_hist))
        if acc is not None:
            chip_sum = chip_sum + acc.astype(jnp.float32)
        acc = lax.ppermute(chip_sum.astype(jnp.bfloat16), "cand", ring(n_cand))
    if n_cand == 1:
        (own_other,) = attend((own_partner,), hist_keys, hist_values, table, (4,), head_dim)
    own_sum = own_mine + lax.ppermute(own_other, "hist", swap(n_hist))
    total = own_sum if acc is None else own_sum + acc.astype(jnp.float32)

    attended = total / length_mine.astype(jnp.float32)
    moments = ring_sum(
        jnp.stack([jnp.sum(attended, axis=-1), jnp.sum(attended * attended, axis=-1)]),
        "head",
        n_head,
    )
    row_mean = moments[0][:, None] / width
    row_square = moments[1][:, None] / width
    normed_out = (attended - row_mean) * lax.rsqrt(row_square - row_mean * row_mean + 1e-05)
    gated = (normed_out * gate_u.astype(jnp.float32)).astype(jnp.bfloat16)
    partial_out = jnp.dot(gated, w_out, preferred_element_type=jnp.float32)
    slice_width = width // n_head
    chunks = partial_out.reshape(row_count, n_head, slice_width).transpose(1, 0, 2)
    summed = ring_reduce_scatter(chunks, "head", n_head, head_index)
    residual = lax.dynamic_slice_in_dim(cand_wide, head_index * slice_width, slice_width, 1)
    row_ids = cand_index * row_count + jnp.arange(row_count, dtype=jnp.int32)
    result = jnp.where((row_ids < count_mine)[:, None], residual + summed, 0.0).astype(jnp.bfloat16)
    result_other = lax.ppermute(result, "hist", swap(n_hist))
    first = jnp.where(first_core, result, result_other)
    second = jnp.where(first_core, result_other, result)
    return jnp.stack([first, second])


def solution(mesh):
    in_specs = (
        P("grp", "cand", None),
        P(None, None, "head"),
        P("head", None),
        P("grp", ("cand", "hist"), "head"),
        P("grp", ("cand", "hist"), "head"),
        P("grp"),
        P("grp"),
    )
    out_specs = P("grp", "cand", "head")
    return jax.shard_map(shards, mesh=mesh, in_specs=in_specs, out_specs=out_specs, check_vma=False)
```

```python
import functools
import math

import jax
import jax.numpy as jnp
from jax import lax
from jax.experimental import pallas as pl
from jax.experimental.pallas import tpu as pltpu
from jax.sharding import PartitionSpec as P

HEADS = 16
LANES = 128


def layer_norm_rows(values, width):
    row_mean = jnp.sum(values, axis=-1, keepdims=True) / width
    row_square = jnp.sum(values * values, axis=-1, keepdims=True) / width
    return (values - row_mean) * lax.rsqrt(row_square - row_mean * row_mean + 1e-05)


def ring(n):
    return [(i, (i + 1) % n) for i in range(n)]


def swap(n):
    return [(i, n - 1 - i) for i in range(n)]


def attend_kernel(limits, *refs, count, offset, head_dim, row_tile, key_tile):
    q_refs = refs[:count]
    k_ref, v_ref = refs[count:count + 2]
    o_refs = refs[count + 2:]
    r = pl.program_id(0)
    kv = pl.program_id(1)
    row_count, width = q_refs[0].shape
    half_scale = 0.5 / math.sqrt(head_dim)

    def compute(q_ref, o_ref, rows, keys_live):
        lane = lax.broadcasted_iota(jnp.int32, (1, LANES), 1)
        column = kv * key_tile + lax.broadcasted_iota(jnp.int32, (1, key_tile), 1)
        valid = column < keys_live

        def pair(p, carry):
            lanes = pl.ds(pl.multiple_of(p * LANES, LANES), LANES)
            q_pair = q_ref[0:rows, lanes]
            k_pair = k_ref[:, lanes]
            v_pair = v_ref[:, lanes]
            heads = LANES // head_dim
            head_of_lane = lane // head_dim
            q_stack = jnp.concatenate(
                [jnp.where(head_of_lane == hh, q_pair, jnp.zeros_like(q_pair)) for hh in range(heads)],
                axis=0,
            )
            scores = lax.dot_general(
                q_stack, k_pair, (((1,), (1,)), ((), ())), preferred_element_type=jnp.float32
            )
            halves = scores * half_scale
            weights = jnp.where(valid, halves + halves * jnp.tanh(halves), 0.0).astype(jnp.bfloat16)
            mixed = jnp.dot(weights, v_pair, preferred_element_type=jnp.float32)
            out = mixed[0:rows]
            for hh in range(1, heads):
                out = jnp.where(head_of_lane == hh, mixed[hh * rows:(hh + 1) * rows], out)
            o_ref[0:rows, lanes] += out
            return carry

        lax.fori_loop(0, width // LANES, pair, 0)

    def request(which, q_ref, o_ref):
        rows_live = limits[offset + 4 * which]
        keys_live = limits[offset + 4 * which + 1]

        @pl.when((r == 0) & (kv == 0))
        def _():
            o_ref[...] = jnp.zeros((row_count, width), jnp.float32)

        live = (r == which) & (kv * key_tile < keys_live)
        if row_count > row_tile:
            pl.when(live & (rows_live > row_tile))(
                lambda: compute(q_ref, o_ref, row_count, keys_live)
            )
            pl.when(live & (rows_live > 0) & (rows_live <= row_tile))(
                lambda: compute(q_ref, o_ref, row_tile, keys_live)
            )
        else:
            pl.when(live & (rows_live > 0))(lambda: compute(q_ref, o_ref, row_count, keys_live))

    for which in range(count):
        request(which, q_refs[which], o_refs[which])


def attend(queries, hist_keys, hist_values, table, offset, head_dim):
    count = len(queries)
    row_count, width = queries[0].shape
    key_count = hist_values.shape[1]
    row_tile = min(128, row_count)
    key_tile = min(1024, key_count)
    key_tiles = key_count // key_tile
    kernel = functools.partial(
        attend_kernel, count=count, offset=offset, head_dim=head_dim, row_tile=row_tile,
        key_tile=key_tile,
    )

    def kv_index(r, kv, lim):
        return (lim[offset + 4 * r + 2], jnp.minimum(kv, lim[offset + 4 * r + 3]), 0)

    flops = 4 * count * row_count * key_count * width
    out = jax.ShapeDtypeStruct((row_count, width), jnp.float32)
    whole = pl.BlockSpec((row_count, width), lambda r, kv, lim: (0, 0))
    return pl.pallas_call(
        kernel,
        out_shape=(out,) * count,
        grid_spec=pltpu.PrefetchScalarGridSpec(
            num_scalar_prefetch=1,
            grid=(count, key_tiles),
            in_specs=[whole] * count + [
                pl.BlockSpec((None, key_tile, width), kv_index),
                pl.BlockSpec((None, key_tile, width), kv_index),
            ],
            out_specs=(whole,) * count,
        ),
        cost_estimate=pl.CostEstimate(
            flops=flops,
            transcendentals=count * row_count * key_count * (width // head_dim),
            bytes_accessed=2 * count * key_count * width * 2 + count * row_count * width * 6,
        ),
    )(table, *queries, hist_keys, hist_values)


def ring_reduce_scatter(chunks, axis, n, index):
    acc = None
    for t in range(1, n):
        part = lax.dynamic_index_in_dim(chunks, (index - t) % n, 0, keepdims=False)
        if acc is not None:
            part = part + acc.astype(jnp.float32)
        acc = lax.ppermute(part.astype(jnp.bfloat16), axis, ring(n))
    own = lax.dynamic_index_in_dim(chunks, index, 0, keepdims=False)
    return own if acc is None else own + acc.astype(jnp.float32)


def ring_sum(values, axis, n):
    total = values
    moving = values
    for _ in range(1, n):
        moving = lax.ppermute(moving, axis, ring(n))
        total = total + moving
    return total


def shards(candidates, w_in, w_out, hist_keys, hist_values, lengths, counts):
    requests, row_count, width = candidates.shape
    width_here = w_in.shape[2]
    head_dim = width // HEADS
    n_cand = lax.axis_size("cand")
    n_hist = lax.axis_size("hist")
    n_head = lax.axis_size("head")
    cand_index = lax.axis_index("cand")
    hist_index = lax.axis_index("hist")
    head_index = lax.axis_index("head")
    assert n_hist == 2 and requests == 2
    first_core = hist_index == 0

    cand_mine = lax.dynamic_index_in_dim(candidates, hist_index, 0, keepdims=False)
    cand_wide = cand_mine.astype(jnp.float32)
    normed = layer_norm_rows(cand_wide, width).astype(jnp.bfloat16)
    projected = jnp.dot(
        normed, w_in.reshape(width, 2 * width_here), preferred_element_type=jnp.float32
    )
    activated = jax.nn.silu(projected).astype(jnp.bfloat16).reshape(row_count, 2, width_here)
    gate_u = activated[:, 0, :]
    query_mine = activated[:, 1, :]

    blocks = hist_keys.shape[1]
    key_base = (cand_index * n_hist + hist_index) * blocks
    length_mine = jnp.where(first_core, lengths[0], lengths[1])
    count_mine = jnp.where(first_core, counts[0], counts[1])
    key_tile = min(1024, blocks)
    key_tiles = blocks // key_tile
    request = jnp.stack([hist_index, 1 - hist_index]).astype(jnp.int32)
    counts_r = jnp.take(counts, request)
    keys_live = jnp.clip(jnp.take(lengths, request) - key_base, 0, blocks)
    last_tile = jnp.clip((keys_live + key_tile - 1) // key_tile - 1, 0, key_tiles - 1)
    row_base = ((cand_index - jnp.arange(n_cand)) % n_cand) * row_count
    rows_live = jnp.clip(counts_r[None, :] - row_base[:, None], 0, row_count)
    table = jnp.stack(
        [
            rows_live,
            jnp.broadcast_to(keys_live, rows_live.shape),
            jnp.broadcast_to(request, rows_live.shape),
            jnp.broadcast_to(last_tile, rows_live.shape),
        ],
        axis=-1,
    ).astype(jnp.int32).reshape(-1)

    own_partner = lax.ppermute(query_mine, "hist", swap(n_hist))
    (own_mine,) = attend((query_mine,), hist_keys, hist_values, table, 0, head_dim)
    acc = None
    forward = query_mine
    previous = own_mine
    for k in range(1, n_cand):
        query_k = lax.ppermute(forward, "cand", ring(n_cand))
        query_k, _ = lax.optimization_barrier((query_k, previous))
        forward = query_k
        query_partner = lax.ppermute(query_k, "hist", swap(n_hist))
        part_mine, part_other = attend(
            (query_k, query_partner), hist_keys, hist_values, table, 8 * k, head_dim
        )
        previous = part_mine
        chip_sum = part_mine + lax.ppermute(part_other, "hist", swap(n_hist))
        if acc is not None:
            chip_sum = chip_sum + acc.astype(jnp.float32)
        acc = lax.ppermute(chip_sum.astype(jnp.bfloat16), "cand", ring(n_cand))
    (own_other,) = attend((own_partner,), hist_keys, hist_values, table, 4, head_dim)
    own_sum = own_mine + lax.ppermute(own_other, "hist", swap(n_hist))
    total = own_sum if acc is None else own_sum + acc.astype(jnp.float32)

    attended = total / length_mine.astype(jnp.float32)
    moments = ring_sum(
        jnp.stack([jnp.sum(attended, axis=-1), jnp.sum(attended * attended, axis=-1)]),
        "head",
        n_head,
    )
    row_mean = moments[0][:, None] / width
    row_square = moments[1][:, None] / width
    normed_out = (attended - row_mean) * lax.rsqrt(row_square - row_mean * row_mean + 1e-05)
    gated = (normed_out * gate_u.astype(jnp.float32)).astype(jnp.bfloat16)
    partial_out = jnp.dot(gated, w_out, preferred_element_type=jnp.float32)
    slice_width = width // n_head
    chunks = partial_out.reshape(row_count, n_head, slice_width).transpose(1, 0, 2)
    summed = ring_reduce_scatter(chunks, "head", n_head, head_index)
    residual = lax.dynamic_slice_in_dim(cand_wide, head_index * slice_width, slice_width, 1)
    row_ids = cand_index * row_count + jnp.arange(row_count, dtype=jnp.int32)
    result = jnp.where((row_ids < count_mine)[:, None], residual + summed, 0.0).astype(jnp.bfloat16)
    result_other = lax.ppermute(result, "hist", swap(n_hist))
    both = jnp.stack([result, result_other])
    return lax.dynamic_slice_in_dim(jnp.concatenate([both, both]), hist_index, 2, 0)


def solution(mesh):
    in_specs = (
        P("grp", "cand", None),
        P(None, None, "head"),
        P("head", None),
        P("grp", ("cand", "hist"), "head"),
        P("grp", ("cand", "hist"), "head"),
        P("grp"),
        P("grp"),
    )
    out_specs = P("grp", "cand", "head")
    return jax.shard_map(shards, mesh=mesh, in_specs=in_specs, out_specs=out_specs, check_vma=False)
```

```python
import functools
import math

import jax
import jax.numpy as jnp
from jax import lax
from jax.experimental import pallas as pl
from jax.experimental.pallas import tpu as pltpu
from jax.sharding import PartitionSpec as P

HEADS = 16
LANES = 128


def layer_norm_rows(values, width):
    row_mean = jnp.sum(values, axis=-1, keepdims=True) / width
    row_square = jnp.sum(values * values, axis=-1, keepdims=True) / width
    return (values - row_mean) * lax.rsqrt(row_square - row_mean * row_mean + 1e-05)


def ring(n):
    return [(i, (i + 1) % n) for i in range(n)]


def swap(n):
    return [(i, n - 1 - i) for i in range(n)]


def attend_kernel(limits, *refs, count, offset, head_dim, row_tile, key_tile):
    q_refs = refs[:count]
    k_ref, v_ref = refs[count:count + 2]
    o_refs = refs[count + 2:]
    r = pl.program_id(0)
    kv = pl.program_id(1)
    row_count, width = q_refs[0].shape
    half_scale = 0.5 / math.sqrt(head_dim)

    def compute(q_ref, o_ref, rows, keys_live):
        lane = lax.broadcasted_iota(jnp.int32, (1, LANES), 1)
        column = kv * key_tile + lax.broadcasted_iota(jnp.int32, (1, key_tile), 1)
        valid = column < keys_live

        def pair(p, carry):
            lanes = pl.ds(pl.multiple_of(p * LANES, LANES), LANES)
            q_pair = q_ref[0:rows, lanes]
            k_pair = k_ref[:, lanes]
            v_pair = v_ref[:, lanes]
            heads = LANES // head_dim
            head_of_lane = lane // head_dim
            q_stack = jnp.concatenate(
                [jnp.where(head_of_lane == hh, q_pair, jnp.zeros_like(q_pair)) for hh in range(heads)],
                axis=0,
            )
            scores = lax.dot_general(
                q_stack, k_pair, (((1,), (1,)), ((), ())), preferred_element_type=jnp.float32
            )
            halves = scores * half_scale
            weights = jnp.where(valid, halves + halves * jnp.tanh(halves), 0.0).astype(jnp.bfloat16)
            mixed = jnp.dot(weights, v_pair, preferred_element_type=jnp.float32)
            out = mixed[0:rows]
            for hh in range(1, heads):
                out = jnp.where(head_of_lane == hh, mixed[hh * rows:(hh + 1) * rows], out)
            o_ref[0:rows, lanes] += out
            return carry

        lax.fori_loop(0, width // LANES, pair, 0)

    def request(which, q_ref, o_ref):
        rows_live = limits[offset + 4 * which]
        keys_live = limits[offset + 4 * which + 1]

        @pl.when((r == 0) & (kv == 0))
        def _():
            o_ref[...] = jnp.zeros((row_count, width), jnp.float32)

        live = (r == which) & (kv * key_tile < keys_live)
        if row_count > row_tile:
            pl.when(live & (rows_live > row_tile))(
                lambda: compute(q_ref, o_ref, row_count, keys_live)
            )
            pl.when(live & (rows_live > 0) & (rows_live <= row_tile))(
                lambda: compute(q_ref, o_ref, row_tile, keys_live)
            )
        else:
            pl.when(live & (rows_live > 0))(lambda: compute(q_ref, o_ref, row_count, keys_live))

    for which in range(count):
        request(which, q_refs[which], o_refs[which])


def attend(queries, hist_keys, hist_values, table, offset, head_dim):
    count = len(queries)
    row_count, width = queries[0].shape
    key_count = hist_values.shape[1]
    row_tile = min(128, row_count)
    key_tile = min(1024, key_count)
    key_tiles = key_count // key_tile
    kernel = functools.partial(
        attend_kernel, count=count, offset=offset, head_dim=head_dim, row_tile=row_tile,
        key_tile=key_tile,
    )

    def kv_index(r, kv, lim):
        return (lim[offset + 4 * r + 2], jnp.minimum(kv, lim[offset + 4 * r + 3]), 0)

    flops = 4 * count * row_count * key_count * width
    out = jax.ShapeDtypeStruct((row_count, width), jnp.float32)
    whole = pl.BlockSpec((row_count, width), lambda r, kv, lim: (0, 0))
    return pl.pallas_call(
        kernel,
        out_shape=(out,) * count,
        grid_spec=pltpu.PrefetchScalarGridSpec(
            num_scalar_prefetch=1,
            grid=(count, key_tiles),
            in_specs=[whole] * count + [
                pl.BlockSpec((None, key_tile, width), kv_index),
                pl.BlockSpec((None, key_tile, width), kv_index),
            ],
            out_specs=(whole,) * count,
        ),
        cost_estimate=pl.CostEstimate(
            flops=flops,
            transcendentals=count * row_count * key_count * (width // head_dim),
            bytes_accessed=2 * count * key_count * width * 2 + count * row_count * width * 6,
        ),
    )(table, *queries, hist_keys, hist_values)


def ring_reduce_scatter(chunks, axis, n, index):
    acc = None
    for t in range(1, n):
        part = lax.dynamic_index_in_dim(chunks, (index - t) % n, 0, keepdims=False)
        if acc is not None:
            part = part + acc.astype(jnp.float32)
        acc = lax.ppermute(part.astype(jnp.bfloat16), axis, ring(n))
    own = lax.dynamic_index_in_dim(chunks, index, 0, keepdims=False)
    return own if acc is None else own + acc.astype(jnp.float32)


def ring_sum(values, axis, n):
    total = values
    moving = values
    for _ in range(1, n):
        moving = lax.ppermute(moving, axis, ring(n))
        total = total + moving
    return total


def shards(candidates, w_in, w_out, hist_keys, hist_values, lengths, counts):
    requests, row_count, width = candidates.shape
    width_here = w_in.shape[2]
    head_dim = width // HEADS
    n_cand = lax.axis_size("cand")
    n_hist = lax.axis_size("hist")
    n_head = lax.axis_size("head")
    cand_index = lax.axis_index("cand")
    hist_index = lax.axis_index("hist")
    head_index = lax.axis_index("head")
    assert n_hist == 2 and requests == 2
    first_core = hist_index == 0

    cand_mine = lax.dynamic_index_in_dim(candidates, hist_index, 0, keepdims=False)
    cand_wide = cand_mine.astype(jnp.float32)
    normed = layer_norm_rows(cand_wide, width).astype(jnp.bfloat16)
    projected = jnp.einsum("cd,dgf->gcf", normed, w_in, preferred_element_type=jnp.float32)
    activated = jax.nn.silu(projected).astype(jnp.bfloat16)
    gate_u = activated[0]
    query_mine = activated[1]

    blocks = hist_keys.shape[1]
    key_base = (cand_index * n_hist + hist_index) * blocks
    length_mine = jnp.where(first_core, lengths[0], lengths[1])
    count_mine = jnp.where(first_core, counts[0], counts[1])
    key_tile = min(1024, blocks)
    key_tiles = blocks // key_tile
    request = jnp.stack([hist_index, 1 - hist_index]).astype(jnp.int32)
    counts_r = jnp.where(first_core, counts, counts[::-1])
    keys_live = jnp.clip(jnp.where(first_core, lengths, lengths[::-1]) - key_base, 0, blocks)
    last_tile = jnp.clip((keys_live + key_tile - 1) // key_tile - 1, 0, key_tiles - 1)
    row_base = ((cand_index - jnp.arange(n_cand)) % n_cand) * row_count
    rows_live = jnp.clip(counts_r[None, :] - row_base[:, None], 0, row_count)
    table = jnp.stack(
        [
            rows_live,
            jnp.broadcast_to(keys_live, rows_live.shape),
            jnp.broadcast_to(request, rows_live.shape),
            jnp.broadcast_to(last_tile, rows_live.shape),
        ],
        axis=-1,
    ).astype(jnp.int32).reshape(-1)

    own_partner = lax.ppermute(query_mine, "hist", swap(n_hist))
    (own_mine,) = attend((query_mine,), hist_keys, hist_values, table, 0, head_dim)
    acc = None
    forward = query_mine
    previous = own_mine
    for k in range(1, n_cand):
        query_k = lax.ppermute(forward, "cand", ring(n_cand))
        query_k, _ = lax.optimization_barrier((query_k, previous))
        forward = query_k
        query_partner = lax.ppermute(query_k, "hist", swap(n_hist))
        part_mine, part_other = attend(
            (query_k, query_partner), hist_keys, hist_values, table, 8 * k, head_dim
        )
        previous = part_mine
        chip_sum = part_mine + lax.ppermute(part_other, "hist", swap(n_hist))
        if acc is not None:
            chip_sum = chip_sum + acc.astype(jnp.float32)
        acc = lax.ppermute(chip_sum.astype(jnp.bfloat16), "cand", ring(n_cand))
    (own_other,) = attend((own_partner,), hist_keys, hist_values, table, 4, head_dim)
    own_sum = own_mine + lax.ppermute(own_other, "hist", swap(n_hist))
    total = own_sum if acc is None else own_sum + acc.astype(jnp.float32)

    attended = total / length_mine.astype(jnp.float32)
    moments = ring_sum(
        jnp.stack([jnp.sum(attended, axis=-1), jnp.sum(attended * attended, axis=-1)]),
        "head",
        n_head,
    )
    row_mean = moments[0][:, None] / width
    row_square = moments[1][:, None] / width
    normed_out = (attended - row_mean) * lax.rsqrt(row_square - row_mean * row_mean + 1e-05)
    gated = (normed_out * gate_u.astype(jnp.float32)).astype(jnp.bfloat16)
    partial_out = jnp.dot(gated, w_out, preferred_element_type=jnp.float32)
    slice_width = width // n_head
    chunks = partial_out.reshape(row_count, n_head, slice_width).transpose(1, 0, 2)
    summed = ring_reduce_scatter(chunks, "head", n_head, head_index)
    residual = lax.dynamic_slice_in_dim(cand_wide, head_index * slice_width, slice_width, 1)
    row_ids = cand_index * row_count + jnp.arange(row_count, dtype=jnp.int32)
    result = jnp.where((row_ids < count_mine)[:, None], residual + summed, 0.0).astype(jnp.bfloat16)
    result_other = lax.ppermute(result, "hist", swap(n_hist))
    both = jnp.stack([result, result_other])
    return lax.dynamic_slice_in_dim(jnp.concatenate([both, both]), hist_index, 2, 0)


def solution(mesh):
    in_specs = (
        P("grp", "cand", None),
        P(None, None, "head"),
        P("head", None),
        P("grp", ("cand", "hist"), "head"),
        P("grp", ("cand", "hist"), "head"),
        P("grp"),
        P("grp"),
    )
    out_specs = P("grp", "cand", "head")
    return jax.shard_map(shards, mesh=mesh, in_specs=in_specs, out_specs=out_specs, check_vma=False)
```

```python
import functools
import math

import jax
import jax.numpy as jnp
from jax import lax
from jax.experimental import pallas as pl
from jax.experimental.pallas import tpu as pltpu
from jax.sharding import PartitionSpec as P

HEADS = 16
LANES = 128


def layer_norm_rows(values, width):
    row_mean = jnp.sum(values, axis=-1, keepdims=True) / width
    row_square = jnp.sum(values * values, axis=-1, keepdims=True) / width
    return (values - row_mean) * lax.rsqrt(row_square - row_mean * row_mean + 1e-05)


def ring(n):
    return [(i, (i + 1) % n) for i in range(n)]


def swap(n):
    return [(i, n - 1 - i) for i in range(n)]


def attend_kernel(limits, *refs, count, offset, head_dim, row_tile, key_tile):
    q_refs = refs[:count]
    k_ref, v_ref = refs[count:count + 2]
    o_refs = refs[count + 2:]
    r = pl.program_id(0)
    kv = pl.program_id(1)
    row_count, width = q_refs[0].shape
    half_scale = 0.5 / math.sqrt(head_dim)

    def compute(q_ref, o_ref, rows, keys_live):
        lane = lax.broadcasted_iota(jnp.int32, (1, LANES), 1)
        column = kv * key_tile + lax.broadcasted_iota(jnp.int32, (1, key_tile), 1)
        valid = column < keys_live

        def pair(p, carry):
            lanes = pl.ds(pl.multiple_of(p * LANES, LANES), LANES)
            q_pair = q_ref[0:rows, lanes]
            k_pair = k_ref[:, lanes]
            v_pair = v_ref[:, lanes]
            heads = LANES // head_dim
            head_of_lane = lane // head_dim
            q_stack = jnp.concatenate(
                [jnp.where(head_of_lane == hh, q_pair, jnp.zeros_like(q_pair)) for hh in range(heads)],
                axis=0,
            )
            scores = lax.dot_general(
                q_stack, k_pair, (((1,), (1,)), ((), ())), preferred_element_type=jnp.float32
            )
            halves = scores * half_scale
            weights = jnp.where(valid, halves + halves * jnp.tanh(halves), 0.0).astype(jnp.bfloat16)
            mixed = jnp.dot(weights, v_pair, preferred_element_type=jnp.float32)
            out = mixed[0:rows]
            for hh in range(1, heads):
                out = jnp.where(head_of_lane == hh, mixed[hh * rows:(hh + 1) * rows], out)
            o_ref[0:rows, lanes] += out
            return carry

        lax.fori_loop(0, width // LANES, pair, 0)

    def request(which, q_ref, o_ref):
        rows_live = limits[offset + 4 * which]
        keys_live = limits[offset + 4 * which + 1]

        @pl.when((r == 0) & (kv == 0))
        def _():
            o_ref[...] = jnp.zeros((row_count, width), jnp.float32)

        live = (r == which) & (kv * key_tile < keys_live)
        if row_count > row_tile:
            pl.when(live & (rows_live > row_tile))(
                lambda: compute(q_ref, o_ref, row_count, keys_live)
            )
            pl.when(live & (rows_live > 0) & (rows_live <= row_tile))(
                lambda: compute(q_ref, o_ref, row_tile, keys_live)
            )
        else:
            pl.when(live & (rows_live > 0))(lambda: compute(q_ref, o_ref, row_count, keys_live))

    for which in range(count):
        request(which, q_refs[which], o_refs[which])


def attend(queries, hist_keys, hist_values, table, offset, head_dim):
    count = len(queries)
    row_count, width = queries[0].shape
    key_count = hist_values.shape[1]
    row_tile = min(128, row_count)
    key_tile = min(1024, key_count)
    key_tiles = key_count // key_tile
    kernel = functools.partial(
        attend_kernel, count=count, offset=offset, head_dim=head_dim, row_tile=row_tile,
        key_tile=key_tile,
    )

    def kv_index(r, kv, lim):
        return (lim[offset + 4 * r + 2], jnp.minimum(kv, lim[offset + 4 * r + 3]), 0)

    flops = 4 * count * row_count * key_count * width
    out = jax.ShapeDtypeStruct((row_count, width), jnp.float32)
    whole = pl.BlockSpec((row_count, width), lambda r, kv, lim: (0, 0))
    return pl.pallas_call(
        kernel,
        out_shape=(out,) * count,
        grid_spec=pltpu.PrefetchScalarGridSpec(
            num_scalar_prefetch=1,
            grid=(count, key_tiles),
            in_specs=[whole] * count + [
                pl.BlockSpec((None, key_tile, width), kv_index),
                pl.BlockSpec((None, key_tile, width), kv_index),
            ],
            out_specs=(whole,) * count,
        ),
        cost_estimate=pl.CostEstimate(
            flops=flops,
            transcendentals=count * row_count * key_count * (width // head_dim),
            bytes_accessed=2 * count * key_count * width * 2 + count * row_count * width * 6,
        ),
    )(table, *queries, hist_keys, hist_values)


def ring_reduce_scatter(chunks, axis, n, index):
    acc = None
    for t in range(1, n):
        part = lax.dynamic_index_in_dim(chunks, (index - t) % n, 0, keepdims=False)
        if acc is not None:
            part = part + acc.astype(jnp.float32)
        acc = lax.ppermute(part.astype(jnp.bfloat16), axis, ring(n))
    own = lax.dynamic_index_in_dim(chunks, index, 0, keepdims=False)
    return own if acc is None else own + acc.astype(jnp.float32)


def ring_sum(values, axis, n):
    total = values
    moving = values
    for _ in range(1, n):
        moving = lax.ppermute(moving, axis, ring(n))
        total = total + moving
    return total


def shards(candidates, w_in, w_out, hist_keys, hist_values, lengths, counts):
    requests, row_count, width = candidates.shape
    width_here = w_in.shape[2]
    head_dim = width // HEADS
    n_cand = lax.axis_size("cand")
    n_hist = lax.axis_size("hist")
    n_head = lax.axis_size("head")
    cand_index = lax.axis_index("cand")
    hist_index = lax.axis_index("hist")
    head_index = lax.axis_index("head")
    assert n_hist == 2 and requests == 2
    first_core = hist_index == 0

    cand_mine = lax.dynamic_index_in_dim(candidates, hist_index, 0, keepdims=False)
    cand_wide = cand_mine.astype(jnp.float32)
    normed = layer_norm_rows(cand_wide, width).astype(jnp.bfloat16)
    projected = jnp.dot(
        normed, w_in.reshape(width, 2 * width_here), preferred_element_type=jnp.float32
    )
    activated = jax.nn.silu(projected).astype(jnp.bfloat16).reshape(row_count, 2, width_here)
    gate_u = activated[:, 0, :]
    query_mine = activated[:, 1, :]

    blocks = hist_keys.shape[1]
    key_base = (cand_index * n_hist + hist_index) * blocks
    length_mine = jnp.where(first_core, lengths[0], lengths[1])
    count_mine = jnp.where(first_core, counts[0], counts[1])
    key_tile = min(1024, blocks)
    key_tiles = blocks // key_tile
    request = jnp.stack([hist_index, 1 - hist_index]).astype(jnp.int32)
    counts_r = jnp.where(first_core, counts, counts[::-1])
    keys_live = jnp.clip(jnp.where(first_core, lengths, lengths[::-1]) - key_base, 0, blocks)
    last_tile = jnp.clip((keys_live + key_tile - 1) // key_tile - 1, 0, key_tiles - 1)
    row_base = ((cand_index - jnp.arange(n_cand)) % n_cand) * row_count
    rows_live = jnp.clip(counts_r[None, :] - row_base[:, None], 0, row_count)
    table = jnp.stack(
        [
            rows_live,
            jnp.broadcast_to(keys_live, rows_live.shape),
            jnp.broadcast_to(request, rows_live.shape),
            jnp.broadcast_to(last_tile, rows_live.shape),
        ],
        axis=-1,
    ).astype(jnp.int32).reshape(-1)

    own_partner = lax.ppermute(query_mine, "hist", swap(n_hist))
    (own_mine,) = attend((query_mine,), hist_keys, hist_values, table, 0, head_dim)
    acc = None
    forward = query_mine
    previous = own_mine
    for k in range(1, n_cand):
        query_k = lax.ppermute(forward, "cand", ring(n_cand))
        query_k, _ = lax.optimization_barrier((query_k, previous))
        forward = query_k
        query_partner = lax.ppermute(query_k, "hist", swap(n_hist))
        part_mine, part_other = attend(
            (query_k, query_partner), hist_keys, hist_values, table, 8 * k, head_dim
        )
        previous = part_mine
        chip_sum = part_mine + lax.ppermute(part_other, "hist", swap(n_hist))
        if acc is not None:
            chip_sum = chip_sum + acc.astype(jnp.float32)
        acc = lax.ppermute(chip_sum.astype(jnp.bfloat16), "cand", ring(n_cand))
    (own_other,) = attend((own_partner,), hist_keys, hist_values, table, 4, head_dim)
    own_sum = own_mine + lax.ppermute(own_other, "hist", swap(n_hist))
    total = own_sum if acc is None else own_sum + acc.astype(jnp.float32)

    attended = total / length_mine.astype(jnp.float32)
    moments = ring_sum(
        jnp.stack([jnp.sum(attended, axis=-1), jnp.sum(attended * attended, axis=-1)]),
        "head",
        n_head,
    )
    row_mean = moments[0][:, None] / width
    row_square = moments[1][:, None] / width
    normed_out = (attended - row_mean) * lax.rsqrt(row_square - row_mean * row_mean + 1e-05)
    gated = (normed_out * gate_u.astype(jnp.float32)).astype(jnp.bfloat16)
    partial_out = jnp.dot(gated, w_out, preferred_element_type=jnp.float32)
    slice_width = width // n_head
    chunks = partial_out.reshape(row_count, n_head, slice_width).transpose(1, 0, 2)
    summed = ring_reduce_scatter(chunks, "head", n_head, head_index)
    residual = lax.dynamic_slice_in_dim(cand_wide, head_index * slice_width, slice_width, 1)
    row_ids = cand_index * row_count + jnp.arange(row_count, dtype=jnp.int32)
    result = jnp.where((row_ids < count_mine)[:, None], residual + summed, 0.0).astype(jnp.bfloat16)
    result_other = lax.ppermute(result, "hist", swap(n_hist))
    both = jnp.stack([result, result_other])
    return lax.dynamic_slice_in_dim(jnp.concatenate([both, both]), hist_index, 2, 0)


def solution(mesh):
    in_specs = (
        P("grp", "cand", None),
        P(None, None, "head"),
        P("head", None),
        P("grp", ("cand", "hist"), "head"),
        P("grp", ("cand", "hist"), "head"),
        P("grp"),
        P("grp"),
    )
    out_specs = P("grp", "cand", "head")
    return jax.shard_map(shards, mesh=mesh, in_specs=in_specs, out_specs=out_specs, check_vma=False)
```
